32 devices in a mesh: member: 2 (over y), vocab: 16 (over z, x, core).
Axes of the slice: x: 2, y: 2, z: 4, core: 2. Of those that a mesh axis runs over, the one named last changes fastest.
Arguments:
- hidden: bfloat16 [2, 512, 2048], P('member', None, 'vocab'), as said below
- norm_gain: bfloat16 [2, 2048], P('member', 'vocab'), may hold values from 0.5 to 1.5
- head: bfloat16 [2, 2048, 64128], P('member', None, 'vocab'), as said below
- pool_weight: float32 [2], P('member'), may hold values from 0.25 to 1
Outputs:
- log_probs: float32 [512, 64128], P('member', 'vocab')
- agreement: float32 [512], P('member')
The draws below stay inside these ranges and needn't reach their ends.
Inputs may be any that keep to these rules, and one draw needn't show every extreme that they name: `hidden`: finite values; every member's row has a root mean square over its 2048 features between 0.1 and 100. `head`: finite values, each at most 60 in magnitude, so that a row's logits may reach about a thousand in magnitude.
All inputs are finite; a program needn't handle non-finite values.
Results may differ from the reference program's by a relative error of at most 0.00052.
Values may be sent and summed in bfloat16 or wider, within the bound.
No kernel may reach another device: no remote copies, remote signals or barrier semaphores. Data moves between devices by JAX's collectives and lax.ppermute only.
A program may use at most 128 MiB of HBM per device.

```python
import math
import jax
import jax.numpy as jnp
from jax import lax

D = 2048
VOCAB = 64128
ROWS = 512
MEMBERS = 2


aligned_rows = 8


def drawn_layout(key):
    columns = jax.random.randint(jax.random.fold_in(key, 11), (MEMBERS, aligned_rows), 0, VOCAB - 1)
    directions = jax.random.truncated_normal(jax.random.fold_in(key, 12), -4.0, 4.0, (MEMBERS, aligned_rows, D), jnp.float32)
    offsets = jax.random.uniform(jax.random.fold_in(key, 13), (MEMBERS, aligned_rows, 1), jnp.float32, 0.0, 1.0)
    order = jax.random.permutation(jax.random.fold_in(key, 14), aligned_rows).astype(jnp.float32)
    target = 150.0 + 750.0 * (order[None, :, None] + offsets) / aligned_rows
    return (columns, directions, target)


def draw_head(key, part):
    shape = (MEMBERS, D, VOCAB)
    base = jax.random.truncated_normal(jax.random.fold_in(key, 1), -4.0, 4.0, shape, jnp.float32)
    spread = jnp.exp(jax.random.uniform(jax.random.fold_in(key, 2), (MEMBERS, 1, VOCAB), jnp.float32, 0.0, math.log(10.0)))
    ramp = 1.0 + 2.0 * jnp.arange(VOCAB, dtype=jnp.float32) / VOCAB
    scale_root = math.sqrt(D)
    matrix = base * spread * ramp[None, None, :] / (3.0 * scale_root)
    columns, directions, target = drawn_layout(key)
    member_ids = jnp.arange(MEMBERS, dtype=jnp.int32)[:, None, None]
    feature_ids = jnp.arange(D, dtype=jnp.int32)[None, None, :]
    column_ids = columns[:, :, None]
    first_values = directions * target / D
    factor = 1.0 - 2.0 / target
    matrix = matrix.at[member_ids, feature_ids, column_ids].set(first_values)
    matrix = matrix.at[member_ids, feature_ids, column_ids + 1].set(first_values * factor)
    return matrix.astype(jnp.bfloat16)


def draw_hidden(key, part):
    shape = (MEMBERS, ROWS, D)
    row_scale = jnp.exp(jax.random.uniform(jax.random.fold_in(key, 3), (MEMBERS, ROWS, 1), jnp.float32, 0.0, math.log(10.0)))
    positions = jnp.arange(D, dtype=jnp.float32) / D
    base = jax.random.truncated_normal(jax.random.fold_in(key, 4), -4.0, 4.0, shape, jnp.float32)
    jitter = jnp.exp(jax.random.uniform(jax.random.fold_in(key, 5), (1, 1, D), jnp.float32, 0.0, math.log(2.0)))
    column_scale = (3.0 ** positions)[None, None, :] * jitter
    states = base * row_scale * column_scale
    columns, directions, target = drawn_layout(key)
    aligned = directions * row_scale[:, :aligned_rows] + 0.1 * base[:, :aligned_rows]
    states = states.at[:, :aligned_rows, :].set(aligned)
    return states.astype(jnp.bfloat16)


def steps_of(own_key, shape, pieces, smallest, top_value):
    def one(axis_at, shards_of):
        heights = jax.random.uniform(jax.random.fold_in(jax.random.fold_in(own_key, 6), axis_at), (shards_of,), jnp.float32, smallest / len(pieces), top_value / len(pieces))
        return jnp.repeat(jnp.exp(heights), shape[axis_at] // shards_of).reshape((-1,) + (1,) * (len(shape) - axis_at - 1))

    factor_of = one(*pieces[0])
    for cut in pieces[1:]:
        factor_of = factor_of * one(*cut)
    return factor_of


def setup_inputs(seed: int = 0) -> dict:
    streams_of = jax.random.split(jax.random.key(seed), 5)
    return {
        "hidden": draw_hidden(jax.random.fold_in(streams_of[4], 71), 0),
        "norm_gain": jnp.clip(1.0 + 0.1 * jax.random.normal(streams_of[1], (MEMBERS, D), jnp.float32), 0.5, 1.5).astype(jnp.bfloat16),
        "head": draw_head(jax.random.fold_in(streams_of[4], 71), 0),
        "pool_weight": jnp.clip(jnp.exp(math.log(1.0) - 1.3862944 * jax.random.uniform(streams_of[3], (MEMBERS,), jnp.float32) ** steps_of(streams_of[3], (MEMBERS,), ((0, 2),), -0.2, 0.2)), 0.25, 1.0),
    }


epsilon = 1e-05

def row_lse(values):
    row_peak = lax.optimization_barrier(jnp.max(values, axis=1))
    summed = lax.optimization_barrier(jnp.sum(jnp.exp(values - row_peak[:, None]), axis=1))
    return row_peak + jnp.log(summed)

def reference(hidden, norm_gain, head, pool_weight):

    def member_term(pooled, index):
        states = hidden[index].astype(jnp.float32)
        mean_square = lax.optimization_barrier(jnp.mean(states * states, axis=1, keepdims=True))
        normed = (states * lax.rsqrt(mean_square + epsilon) * norm_gain[index].astype(jnp.float32)[None, :]).astype(jnp.bfloat16)
        logits = jnp.dot(normed, head[index], preferred_element_type=jnp.float32)
        member_lse = row_lse(logits)
        return (pooled + pool_weight[index] * (logits - member_lse[:, None]), None)
    start_pool = jnp.zeros((ROWS, VOCAB), jnp.float32)
    pooled, unused = lax.scan(member_term, start_pool, jnp.arange(MEMBERS, dtype=jnp.int32))
    agreement = row_lse(pooled)
    return (pooled - agreement[:, None], agreement)
```

```python
import jax
import jax.numpy as jnp
from jax import lax
from jax.sharding import PartitionSpec as P

epsilon = 1e-05


def combine_stats(stats):
    peaks = stats[:, 0, :]
    sums = stats[:, 1, :]
    row_peak = jnp.max(peaks, axis=0)
    summed = jnp.sum(sums * jnp.exp(peaks - row_peak[None, :]), axis=0)
    return row_peak, summed


def local_stats(values):
    local_peak = jnp.max(values, axis=1)
    local_sum = jnp.sum(jnp.exp(values - local_peak[:, None]), axis=1)
    return jnp.stack([local_peak, local_sum])


def on_device(hidden, norm_gain, head, pool_weight):
    members = lax.axis_size("member")
    shards = lax.axis_size("vocab")
    me = lax.axis_index("member")
    states = hidden[0]
    row_count, width = states.shape
    share = row_count // members
    weights = head[0]
    vocab_local = weights.shape[1]

    packed = jnp.concatenate([states, norm_gain], axis=0)
    gathered = lax.all_gather(packed, "vocab", axis=0, tiled=False)
    full_states = gathered[:, :row_count, :].astype(jnp.float32)
    gain = gathered[:, row_count, :].astype(jnp.float32)
    width_all = width * shards
    mean_square = jnp.sum(full_states * full_states, axis=(0, 2)) / width_all
    scaling = lax.rsqrt(mean_square + epsilon)
    normed = (full_states * scaling[None, :, None] * gain[:, None, :]).astype(jnp.bfloat16)
    normed = jnp.transpose(normed, (1, 0, 2)).reshape(row_count, width_all)
    logits = jnp.dot(normed, weights, preferred_element_type=jnp.float32)

    w = pool_weight[0]
    own = w * lax.dynamic_slice_in_dim(logits, me * share, share, 0)
    pooled_raw = own
    for shift in range(1, members):
        target = (me + shift) % members
        outgoing = w * lax.dynamic_slice_in_dim(logits, target * share, share, 0)
        perm = [(g, (g + shift) % members) for g in range(members)]
        pooled_raw = pooled_raw + lax.ppermute(outgoing, "member", perm)

    member_stats = lax.all_gather(local_stats(logits), "vocab", axis=0, tiled=False)
    peak, summed = combine_stats(member_stats)
    member_lse = peak + jnp.log(summed)
    offsets = lax.all_gather(w * member_lse, "member", axis=0, tiled=False)
    offset = jnp.sum(lax.dynamic_slice_in_dim(offsets, me * share, share, 1), axis=0)

    pooled = pooled_raw - offset[:, None]
    pooled_stats = lax.all_gather(local_stats(pooled), "vocab", axis=0, tiled=False)
    peak, summed = combine_stats(pooled_stats)
    agreement = peak + jnp.log(summed)
    return (pooled - agreement[:, None], agreement)


def solution(mesh):
    in_specs = (
        P("member", None, "vocab"),
        P("member", "vocab"),
        P("member", None, "vocab"),
        P("member"),
    )
    out_specs = (P("member", "vocab"), P("member"))
    return jax.shard_map(
        on_device, mesh=mesh, in_specs=in_specs, out_specs=out_specs, check_vma=False
    )
```

```python
import jax
import jax.numpy as jnp
from jax import lax
from jax.sharding import PartitionSpec as P

epsilon = 1e-05
send_pieces = 2


def local_stats(values):
    local_peak = jnp.max(values, axis=1)
    local_sum = jnp.sum(jnp.exp(values - local_peak[:, None]), axis=1)
    return jnp.stack([local_peak, local_sum])


def reduce_stats(stats, axis):
    size = lax.axis_size(axis)
    if size & (size - 1):
        gathered = lax.all_gather(stats, axis, axis=0, tiled=False)
        peak = jnp.max(gathered[:, 0], axis=0)
        summed = jnp.sum(gathered[:, 1] * jnp.exp(gathered[:, 0] - peak[None]), axis=0)
        return peak, summed
    distance = 1
    while distance < size:
        perm = [(a, a ^ distance) for a in range(size)]
        other = lax.ppermute(stats, axis, perm)
        peak = jnp.maximum(stats[0], other[0])
        summed = stats[1] * jnp.exp(stats[0] - peak) + other[1] * jnp.exp(other[0] - peak)
        stats = jnp.stack([peak, summed])
        distance *= 2
    return stats[0], stats[1]


def on_device(hidden, norm_gain, head, pool_weight):
    members = lax.axis_size("member")
    shards = lax.axis_size("vocab")
    me = lax.axis_index("member")
    states = hidden[0]
    row_count, width = states.shape
    share = row_count // members
    weights = head[0]
    width_all = width * shards
    member_weights = lax.all_gather(pool_weight, "member", axis=0, tiled=True)
    member_weights, states = lax.optimization_barrier((member_weights, states))

    def logits_of(first_row, rows):
        piece = lax.dynamic_slice_in_dim(states, first_row, rows, 0)
        packed = jnp.concatenate([piece, norm_gain], axis=0)
        gathered = lax.all_gather(packed, "vocab", axis=0, tiled=False)
        full_states = gathered[:, :rows, :].astype(jnp.float32)
        gain = gathered[:, rows, :].astype(jnp.float32)
        mean_square = jnp.sum(full_states * full_states, axis=(0, 2)) / width_all
        scaling = lax.rsqrt(mean_square + epsilon)
        normed = (full_states * scaling[None, :, None] * gain[:, None, :]).astype(jnp.bfloat16)
        normed = jnp.transpose(normed, (1, 0, 2)).reshape(rows, width_all)
        return jnp.dot(normed, weights, preferred_element_type=jnp.float32)

    sub = share // send_pieces
    received = []
    for shift in range(1, members):
        target = (me + shift) % members
        perm = [(g, (g + shift) % members) for g in range(members)]
        parts = []
        for k in range(send_pieces):
            logits = logits_of(target * share + k * sub, sub)
            parts.append(lax.ppermute(logits, "member", perm))
        received.append((member_weights[(me - shift) % members], parts))
    own_logits = logits_of(me * share, share)
    own_weight = member_weights[me]

    pooled_raw = []
    stats = [[] for _ in range(members + 1)]
    for k in range(send_pieces):
        own = own_logits[k * sub:(k + 1) * sub]
        total = own_weight * own
        stats[0].append(local_stats(own))
        for index, (weight, parts) in enumerate(received):
            total = total + weight * parts[k]
            stats[index + 1].append(local_stats(parts[k]))
        pooled_raw.append(total)
        stats[members].append(local_stats(total))
    stats = jnp.stack([jnp.concatenate(column, axis=1) for column in stats], axis=1)
    peak, summed = reduce_stats(stats, "vocab")
    lse = peak + jnp.log(summed)
    offset = own_weight * lse[0]
    for index, (weight, parts) in enumerate(received):
        offset = offset + weight * lse[index + 1]

    agreement = lse[members] - offset
    pooled = jnp.concatenate(pooled_raw, axis=0) - offset[:, None]
    return (pooled - agreement[:, None], agreement)


def solution(mesh):
    in_specs = (
        P("member", None, "vocab"),
        P("member", "vocab"),
        P("member", None, "vocab"),
        P("member"),
    )
    out_specs = (P("member", "vocab"), P("member"))
    return jax.shard_map(
        on_device, mesh=mesh, in_specs=in_specs, out_specs=out_specs, check_vma=False
    )
```

```python
import jax
import jax.numpy as jnp
from jax import lax
from jax.sharding import PartitionSpec as P

epsilon = 1e-05
send_pieces = 2


def local_stats(values):
    local_peak = jnp.max(values, axis=1)
    local_sum = jnp.sum(jnp.exp(values - local_peak[:, None]), axis=1)
    return jnp.stack([local_peak, local_sum])


def reduce_stats(stats, axis):
    size = lax.axis_size(axis)
    if size & (size - 1):
        gathered = lax.all_gather(stats, axis, axis=0, tiled=False)
        peak = jnp.max(gathered[:, 0], axis=0)
        summed = jnp.sum(gathered[:, 1] * jnp.exp(gathered[:, 0] - peak[None]), axis=0)
        return peak, summed
    distance = 1
    while distance < size:
        perm = [(a, a ^ distance) for a in range(size)]
        other = lax.ppermute(stats, axis, perm)
        peak = jnp.maximum(stats[0], other[0])
        summed = stats[1] * jnp.exp(stats[0] - peak) + other[1] * jnp.exp(other[0] - peak)
        stats = jnp.stack([peak, summed])
        distance *= 2
    return stats[0], stats[1]


def on_device(hidden, norm_gain, head, pool_weight):
    members = lax.axis_size("member")
    shards = lax.axis_size("vocab")
    me = lax.axis_index("member")
    states = hidden[0]
    row_count, width = states.shape
    share = row_count // members
    weights = head[0]
    width_all = width * shards
    def logits_of(first_row, rows):
        piece = lax.dynamic_slice_in_dim(states, first_row, rows, 0)
        packed = jnp.concatenate([piece, norm_gain], axis=0)
        gathered = lax.all_gather(packed, "vocab", axis=0, tiled=False)
        full_states = gathered[:, :rows, :].astype(jnp.float32)
        gain = gathered[:, rows, :].astype(jnp.float32)
        mean_square = jnp.sum(full_states * full_states, axis=(0, 2)) / width_all
        scaling = lax.rsqrt(mean_square + epsilon)
        normed = (full_states * scaling[None, :, None] * gain[:, None, :]).astype(jnp.bfloat16)
        normed = jnp.transpose(normed, (1, 0, 2)).reshape(rows, width_all)
        return jnp.dot(normed, weights, preferred_element_type=jnp.float32)

    w = pool_weight[0]
    sub = share // send_pieces
    received = []
    notes = []
    for shift in range(1, members):
        target = (me + shift) % members
        perm = [(g, (g + shift) % members) for g in range(members)]
        parts = []
        piece_stats = []
        for k in range(send_pieces):
            logits = logits_of(target * share + k * sub, sub)
            parts.append(lax.ppermute(w * logits, "member", perm))
            piece_stats.append(local_stats(logits))
        stats_rows = jnp.concatenate(piece_stats, axis=1)
        note = jnp.concatenate([stats_rows, jnp.broadcast_to(w, (1, share))], axis=0)
        received.append(parts)
        notes.append((perm, note))
    own_logits = logits_of(me * share, share)
    notes, own_logits = lax.optimization_barrier(([note for _, note in notes], own_logits))
    notes = [lax.ppermute(note, "member", [(g, (g + shift) % members) for g in range(members)])
             for shift, note in zip(range(1, members), notes)]

    pooled_raw = []
    stats = []
    for k in range(send_pieces):
        own = own_logits[k * sub:(k + 1) * sub]
        total = w * own
        for parts in received:
            total = total + parts[k]
        pooled_raw.append(total)
        stats.append(jnp.stack([local_stats(own), local_stats(total)], axis=1))
    stats = jnp.concatenate(stats, axis=2)
    stats = jnp.concatenate([stats] + [note[:2, None, :] for note in notes], axis=1)
    peak, summed = reduce_stats(stats, "vocab")
    lse = peak + jnp.log(summed)
    offset = w * lse[0]
    for index, note in enumerate(notes):
        offset = offset + note[2] * lse[index + 2]

    agreement = lse[1] - offset
    pooled = jnp.concatenate(pooled_raw, axis=0) - offset[:, None]
    return (pooled - agreement[:, None], agreement)


def solution(mesh):
    in_specs = (
        P("member", None, "vocab"),
        P("member", "vocab"),
        P("member", None, "vocab"),
        P("member"),
    )
    out_specs = (P("member", "vocab"), P("member"))
    return jax.shard_map(
        on_device, mesh=mesh, in_specs=in_specs, out_specs=out_specs, check_vma=False
    )
```

```python
import jax
import jax.numpy as jnp
from jax import lax
from jax.sharding import PartitionSpec as P

epsilon = 1e-05


def local_stats(values):
    local_peak = jnp.max(values, axis=1)
    local_sum = jnp.sum(jnp.exp(values - local_peak[:, None]), axis=1)
    return jnp.stack([local_peak, local_sum])


def reduce_stats(stats, axis):
    size = lax.axis_size(axis)
    if size & (size - 1):
        gathered = lax.all_gather(stats, axis, axis=0, tiled=False)
        peak = jnp.max(gathered[:, 0], axis=0)
        summed = jnp.sum(gathered[:, 1] * jnp.exp(gathered[:, 0] - peak[None]), axis=0)
        return peak, summed
    distance = 1
    while distance < size:
        perm = [(a, a ^ distance) for a in range(size)]
        other = lax.ppermute(stats, axis, perm)
        peak = jnp.maximum(stats[0], other[0])
        summed = stats[1] * jnp.exp(stats[0] - peak) + other[1] * jnp.exp(other[0] - peak)
        stats = jnp.stack([peak, summed])
        distance *= 2
    return stats[0], stats[1]


def on_device(hidden, norm_gain, head, pool_weight):
    members = lax.axis_size("member")
    shards = lax.axis_size("vocab")
    me = lax.axis_index("member")
    states = hidden[0]
    row_count, width = states.shape
    share = row_count // members
    weights = head[0]
    width_all = width * shards
    def logits_of(source, first_row, rows):
        piece = lax.dynamic_slice_in_dim(source, first_row, rows, 0)
        packed = jnp.concatenate([piece, norm_gain], axis=0)
        gathered = lax.all_gather(packed, "vocab", axis=0, tiled=False)
        full_states = gathered[:, :rows, :].astype(jnp.float32)
        gain = gathered[:, rows, :].astype(jnp.float32)
        mean_square = jnp.sum(full_states * full_states, axis=(0, 2)) / width_all
        scaling = lax.rsqrt(mean_square + epsilon)
        normed = (full_states * scaling[None, :, None] * gain[:, None, :]).astype(jnp.bfloat16)
        normed = jnp.transpose(normed, (1, 0, 2)).reshape(rows, width_all)
        return jnp.dot(normed, weights, preferred_element_type=jnp.float32)

    w = pool_weight[0]
    first = share // 4
    second = (share - first) // 2
    sizes = [first, second, share - first - second]
    starts = [sum(sizes[:k]) for k in range(len(sizes))]
    received = []
    notes = []
    first_logits = None
    for shift in range(1, members):
        target = (me + shift) % members
        perm = [(g, (g + shift) % members) for g in range(members)]
        parts = []
        piece_stats = []
        for begin, rows in zip(starts, sizes):
            logits = logits_of(states, target * share + begin, rows)
            if first_logits is None:
                first_logits = logits
            parts.append(lax.ppermute(logits, "member", perm))
            piece_stats.append(local_stats(logits))
        stats_rows = jnp.concatenate(piece_stats, axis=1)
        note = jnp.concatenate([stats_rows, jnp.broadcast_to(w, (1, share))], axis=0)
        received.append(parts)
        notes.append(note)
    first_logits, own_states = lax.optimization_barrier((first_logits, states))
    own_logits = logits_of(own_states, me * share, share)
    notes, own_logits = lax.optimization_barrier((notes, own_logits))
    notes = [lax.ppermute(note, "member", [(g, (g + shift) % members) for g in range(members)])
             for shift, note in zip(range(1, members), notes)]

    pooled_raw = []
    stats = []
    for k, (begin, rows) in enumerate(zip(starts, sizes)):
        own = own_logits[begin:begin + rows]
        total = w * own
        for parts, note in zip(received, notes):
            total = total + note[2, begin:begin + rows, None] * parts[k]
        pooled_raw.append(total)
        stats.append(jnp.stack([local_stats(own), local_stats(total)], axis=1))
    stats = jnp.concatenate(stats, axis=2)
    stats = jnp.concatenate([stats] + [note[:2, None, :] for note in notes], axis=1)
    peak, summed = reduce_stats(stats, "vocab")
    lse = peak + jnp.log(summed)
    offset = w * lse[0]
    for index, note in enumerate(notes):
        offset = offset + note[2] * lse[index + 2]

    agreement = lse[1] - offset
    pooled = jnp.concatenate(pooled_raw, axis=0) - offset[:, None]
    return (pooled - agreement[:, None], agreement)


def solution(mesh):
    in_specs = (
        P("member", None, "vocab"),
        P("member", "vocab"),
        P("member", None, "vocab"),
        P("member"),
    )
    out_specs = (P("member", "vocab"), P("member"))
    return jax.shard_map(
        on_device, mesh=mesh, in_specs=in_specs, out_specs=out_specs, check_vma=False
    )
```

```python
import jax
import jax.numpy as jnp
from jax import lax
from jax.sharding import PartitionSpec as P

epsilon = 1e-05
send_pieces = 2


def local_stats(values):
    local_peak = jnp.max(values, axis=1)
    local_sum = jnp.sum(jnp.exp(values - local_peak[:, None]), axis=1)
    return jnp.stack([local_peak, local_sum])


def reduce_stats(stats, axis):
    size = lax.axis_size(axis)
    if size & (size - 1):
        gathered = lax.all_gather(stats, axis, axis=0, tiled=False)
        peak = jnp.max(gathered[:, 0], axis=0)
        summed = jnp.sum(gathered[:, 1] * jnp.exp(gathered[:, 0] - peak[None]), axis=0)
        return peak, summed
    distance = 1
    while distance < size:
        perm = [(a, a ^ distance) for a in range(size)]
        other = lax.ppermute(stats, axis, perm)
        peak = jnp.maximum(stats[0], other[0])
        summed = stats[1] * jnp.exp(stats[0] - peak) + other[1] * jnp.exp(other[0] - peak)
        stats = jnp.stack([peak, summed])
        distance *= 2
    return stats[0], stats[1]


def gather_shards(x, axis):
    size = lax.axis_size(axis)
    if size & (size - 1):
        return lax.all_gather(x, axis, axis=0, tiled=False)
    index = lax.axis_index(axis)
    block = x[None]
    distance = 1
    while distance < size:
        other = lax.ppermute(block, axis, [(a, a ^ distance) for a in range(size)])
        lower = (index // distance) % 2 == 0
        block = jnp.where(lower, jnp.concatenate([block, other]), jnp.concatenate([other, block]))
        distance *= 2
    return block


def on_device(hidden, norm_gain, head, pool_weight):
    members = lax.axis_size("member")
    shards = lax.axis_size("vocab")
    me = lax.axis_index("member")
    states = hidden[0]
    row_count, width = states.shape
    share = row_count // members
    weights = head[0]
    width_all = width * shards
    def logits_of(first_row, rows, gather):
        piece = lax.dynamic_slice_in_dim(states, first_row, rows, 0)
        packed = jnp.concatenate([piece, norm_gain], axis=0)
        gathered = gather(packed)
        full_states = gathered[:, :rows, :].astype(jnp.float32)
        gain = gathered[:, rows, :].astype(jnp.float32)
        mean_square = jnp.sum(full_states * full_states, axis=(0, 2)) / width_all
        scaling = lax.rsqrt(mean_square + epsilon)
        normed = (full_states * scaling[None, :, None] * gain[:, None, :]).astype(jnp.bfloat16)
        normed = jnp.transpose(normed, (1, 0, 2)).reshape(rows, width_all)
        return jnp.dot(normed, weights, preferred_element_type=jnp.float32)

    w = pool_weight[0]
    sub = share // send_pieces
    received = []
    notes = []
    for shift in range(1, members):
        target = (me + shift) % members
        perm = [(g, (g + shift) % members) for g in range(members)]
        parts = []
        piece_stats = []
        for k in range(send_pieces):
            logits = logits_of(target * share + k * sub, sub, lambda x: gather_shards(x, "vocab"))
            parts.append(lax.ppermute(w * logits, "member", perm))
            piece_stats.append(local_stats(logits))
        stats_rows = jnp.concatenate(piece_stats, axis=1)
        note = jnp.concatenate([stats_rows, jnp.broadcast_to(w, (1, share))], axis=0)
        received.append(parts)
        notes.append((perm, note))
    own_logits = logits_of(me * share, share, lambda x: lax.all_gather(x, "vocab", axis=0, tiled=False))
    notes, own_logits = lax.optimization_barrier(([note for _, note in notes], own_logits))
    notes = [lax.ppermute(note, "member", [(g, (g + shift) % members) for g in range(members)])
             for shift, note in zip(range(1, members), notes)]

    pooled_raw = []
    stats = []
    for k in range(send_pieces):
        own = own_logits[k * sub:(k + 1) * sub]
        total = w * own
        for parts in received:
            total = total + parts[k]
        pooled_raw.append(total)
        stats.append(jnp.stack([local_stats(own), local_stats(total)], axis=1))
    stats = jnp.concatenate(stats, axis=2)
    stats = jnp.concatenate([stats] + [note[:2, None, :] for note in notes], axis=1)
    peak, summed = reduce_stats(stats, "vocab")
    lse = peak + jnp.log(summed)
    offset = w * lse[0]
    for index, note in enumerate(notes):
        offset = offset + note[2] * lse[index + 2]

    agreement = lse[1] - offset
    pooled = jnp.concatenate(pooled_raw, axis=0) - offset[:, None]
    return (pooled - agreement[:, None], agreement)


def solution(mesh):
    in_specs = (
        P("member", None, "vocab"),
        P("member", "vocab"),
        P("member", None, "vocab"),
        P("member"),
    )
    out_specs = (P("member", "vocab"), P("member"))
    return jax.shard_map(
        on_device, mesh=mesh, in_specs=in_specs, out_specs=out_specs, check_vma=False
    )
```

```python
import jax
import jax.numpy as jnp
from jax import lax
from jax.sharding import PartitionSpec as P

epsilon = 1e-05
send_pieces = 2


def local_stats(values):
    local_peak = jnp.max(values, axis=1)
    local_sum = jnp.sum(jnp.exp(values - local_peak[:, None]), axis=1)
    return jnp.stack([local_peak, local_sum])


def reduce_stats(stats, axis):
    size = lax.axis_size(axis)
    if size & (size - 1):
        gathered = lax.all_gather(stats, axis, axis=0, tiled=False)
        peak = jnp.max(gathered[:, 0], axis=0)
        summed = jnp.sum(gathered[:, 1] * jnp.exp(gathered[:, 0] - peak[None]), axis=0)
        return peak, summed
    distance = 1
    while distance < size:
        perm = [(a, a ^ distance) for a in range(size)]
        other = lax.ppermute(stats, axis, perm)
        peak = jnp.maximum(stats[0], other[0])
        summed = stats[1] * jnp.exp(stats[0] - peak) + other[1] * jnp.exp(other[0] - peak)
        stats = jnp.stack([peak, summed])
        distance *= 2
    return stats[0], stats[1]


def on_device(hidden, norm_gain, head, pool_weight):
    members = lax.axis_size("member")
    shards = lax.axis_size("vocab")
    me = lax.axis_index("member")
    states = hidden[0]
    row_count, width = states.shape
    share = row_count // members
    weights = head[0]
    width_all = width * shards
    def logits_of(first_row, rows):
        piece = lax.dynamic_slice_in_dim(states, first_row, rows, 0)
        packed = jnp.concatenate([piece, norm_gain], axis=0)
        gathered = lax.all_gather(packed, "vocab", axis=0, tiled=False)
        full_states = gathered[:, :rows, :].astype(jnp.float32)
        gain = gathered[:, rows, :].astype(jnp.float32)
        mean_square = jnp.sum(full_states * full_states, axis=(0, 2)) / width_all
        scaling = lax.rsqrt(mean_square + epsilon)
        normed = (full_states * scaling[None, :, None] * gain[:, None, :]).astype(jnp.bfloat16)
        normed = jnp.transpose(normed, (1, 0, 2)).reshape(rows, width_all)
        return jnp.dot(normed, weights, preferred_element_type=jnp.float32)

    w = pool_weight[0]
    sub = share // send_pieces
    received = []
    notes = []
    for shift in range(1, members):
        target = (me + shift) % members
        perm = [(g, (g + shift) % members) for g in range(members)]
        parts = []
        piece_stats = []
        for k in range(send_pieces):
            logits = logits_of(target * share + k * sub, sub)
            parts.append(lax.ppermute(w * logits, "member", perm))
            piece_stats.append(local_stats(logits))
        stats_rows = jnp.concatenate(piece_stats, axis=1)
        note = jnp.concatenate([stats_rows, jnp.broadcast_to(w, (1, share))], axis=0)
        received.append(parts)
        notes.append((perm, note))
    own_logits = jnp.concatenate(
        [logits_of(me * share + k * sub, sub) for k in range(send_pieces)], axis=0)
    notes, own_logits = lax.optimization_barrier(([note for _, note in notes], own_logits))
    notes = [lax.ppermute(note, "member", [(g, (g + shift) % members) for g in range(members)])
             for shift, note in zip(range(1, members), notes)]

    pooled_raw = []
    stats = []
    for k in range(send_pieces):
        own = own_logits[k * sub:(k + 1) * sub]
        total = w * own
        for parts in received:
            total = total + parts[k]
        pooled_raw.append(total)
        stats.append(jnp.stack([local_stats(own), local_stats(total)], axis=1))
    stats = jnp.concatenate(stats, axis=2)
    stats = jnp.concatenate([stats] + [note[:2, None, :] for note in notes], axis=1)
    peak, summed = reduce_stats(stats, "vocab")
    lse = peak + jnp.log(summed)
    offset = w * lse[0]
    for index, note in enumerate(notes):
        offset = offset + note[2] * lse[index + 2]

    agreement = lse[1] - offset
    pooled = jnp.concatenate(pooled_raw, axis=0) - offset[:, None]
    return (pooled - agreement[:, None], agreement)


def solution(mesh):
    in_specs = (
        P("member", None, "vocab"),
        P("member", "vocab"),
        P("member", None, "vocab"),
        P("member"),
    )
    out_specs = (P("member", "vocab"), P("member"))
    return jax.shard_map(
        on_device, mesh=mesh, in_specs=in_specs, out_specs=out_specs, check_vma=False
    )
```

```python
import jax
import jax.numpy as jnp
from jax import lax
from jax.sharding import PartitionSpec as P

epsilon = 1e-05
send_pieces = 2
gather_rows = 255


def local_stats(values):
    local_peak = jnp.max(values, axis=1)
    local_sum = jnp.sum(jnp.exp(values - local_peak[:, None]), axis=1)
    return jnp.stack([local_peak, local_sum])


def reduce_stats(stats, axis):
    size = lax.axis_size(axis)
    if size & (size - 1):
        gathered = lax.all_gather(stats, axis, axis=0, tiled=False)
        peak = jnp.max(gathered[:, 0], axis=0)
        summed = jnp.sum(gathered[:, 1] * jnp.exp(gathered[:, 0] - peak[None]), axis=0)
        return peak, summed
    distance = 1
    while distance < size:
        perm = [(a, a ^ distance) for a in range(size)]
        other = lax.ppermute(stats, axis, perm)
        peak = jnp.maximum(stats[0], other[0])
        summed = stats[1] * jnp.exp(stats[0] - peak) + other[1] * jnp.exp(other[0] - peak)
        stats = jnp.stack([peak, summed])
        distance *= 2
    return stats[0], stats[1]


def on_device(hidden, norm_gain, head, pool_weight):
    members = lax.axis_size("member")
    shards = lax.axis_size("vocab")
    me = lax.axis_index("member")
    states = hidden[0]
    row_count, width = states.shape
    share = row_count // members
    weights = head[0]
    width_all = width * shards
    w = pool_weight[0]
    sub = share // send_pieces

    blocks = []
    for shift in range(1, members):
        target = (me + shift) % members
        for k in range(send_pieces):
            blocks.append(lax.dynamic_slice_in_dim(states, target * share + k * sub, sub, 0))
    blocks.append(lax.dynamic_slice_in_dim(states, me * share, share, 0))
    ordered = jnp.concatenate(blocks, axis=0)

    bounds = [0, sub]
    while bounds[-1] < row_count:
        bounds.append(min(bounds[-1] + gather_rows, row_count))
    gain = None

    def normalize(lo, hi, source):
        nonlocal gain
        packed = source[lo:hi]
        if gain is None:
            packed = jnp.concatenate([packed, norm_gain], axis=0)
        gathered = lax.all_gather(packed, "vocab", axis=0, tiled=False)
        if gain is None:
            gain = gathered[:, hi - lo, :].astype(jnp.float32)
        full_states = gathered[:, :hi - lo, :].astype(jnp.float32)
        mean_square = jnp.sum(full_states * full_states, axis=(0, 2)) / width_all
        scaling = lax.rsqrt(mean_square + epsilon)
        piece = (full_states * scaling[None, :, None] * gain[:, None, :]).astype(jnp.bfloat16)
        return jnp.transpose(piece, (1, 0, 2)).reshape(hi - lo, width_all)

    first_normed = normalize(bounds[0], bounds[1], ordered)
    first_logits = jnp.dot(first_normed, weights, preferred_element_type=jnp.float32)
    first_sent = w * first_logits
    first_sent, ordered = lax.optimization_barrier((first_sent, ordered))
    normed = jnp.concatenate(
        [first_normed] + [normalize(lo, hi, ordered) for lo, hi in zip(bounds[1:-1], bounds[2:])], axis=0)

    def logits_of(lo, rows):
        return jnp.dot(normed[lo:lo + rows], weights, preferred_element_type=jnp.float32)

    received = []
    sent = []
    for shift in range(1, members):
        perm = [(g, (g + shift) % members) for g in range(members)]
        parts = []
        for k in range(send_pieces):
            if shift == 1 and k == 0:
                logits, outgoing = first_logits, first_sent
            else:
                logits = logits_of(((shift - 1) * send_pieces + k) * sub, sub)
                outgoing = w * logits
            parts.append(lax.ppermute(outgoing, "member", perm))
            sent.append(logits)
        received.append(parts)
    own_logits = logits_of(row_count - share, share)

    sent, own_logits = lax.optimization_barrier((sent, own_logits))
    notes = []
    for shift in range(1, members):
        piece_stats = [local_stats(x) for x in sent[(shift - 1) * send_pieces:shift * send_pieces]]
        note = jnp.concatenate(
            [jnp.concatenate(piece_stats, axis=1), jnp.broadcast_to(w, (1, share))], axis=0)
        perm = [(g, (g + shift) % members) for g in range(members)]
        notes.append(lax.ppermute(note, "member", perm))

    def piece_terms(k):
        own = own_logits[k * sub:(k + 1) * sub]
        total = w * own
        for parts in received:
            total = total + parts[k]
        return total, jnp.concatenate([local_stats(own), local_stats(total)], axis=1)

    def flat_lse(stats):
        peak, summed = reduce_stats(stats[:, None, :], "vocab")
        return (peak + jnp.log(summed))[0]

    early = [piece_terms(k) for k in range(send_pieces - 1)]
    early_lse = flat_lse(jnp.concatenate([stats for _, stats in early], axis=1))
    last_parts = [parts[-1] for parts in received]
    last_parts, early_lse = lax.optimization_barrier((last_parts, early_lse))
    for parts, part in zip(received, last_parts):
        parts[-1] = part
    last_total, last_stats = piece_terms(send_pieces - 1)
    tail = jnp.concatenate([last_stats] + [note[:2] for note in notes], axis=1)
    tail_lse = flat_lse(tail)

    own_lse = []
    pooled_lse = []
    for k in range(send_pieces - 1):
        own_lse.append(early_lse[2 * k * sub:(2 * k + 1) * sub])
        pooled_lse.append(early_lse[(2 * k + 1) * sub:(2 * k + 2) * sub])
    own_lse.append(tail_lse[:sub])
    pooled_lse.append(tail_lse[sub:2 * sub])
    offset = w * jnp.concatenate(own_lse)
    for index, note in enumerate(notes):
        lo = 2 * sub + index * share
        offset = offset + note[2] * tail_lse[lo:lo + share]

    agreement = jnp.concatenate(pooled_lse) - offset
    pooled_raw = jnp.concatenate([total for total, _ in early] + [last_total], axis=0)
    pooled = pooled_raw - offset[:, None]
    return (pooled - agreement[:, None], agreement)


def solution(mesh):
    in_specs = (
        P("member", None, "vocab"),
        P("member", "vocab"),
        P("member", None, "vocab"),
        P("member"),
    )
    out_specs = (P("member", "vocab"), P("member"))
    return jax.shard_map(
        on_device, mesh=mesh, in_specs=in_specs, out_specs=out_specs, check_vma=False
    )
```

```python
import jax
import jax.numpy as jnp
from jax import lax
from jax.sharding import PartitionSpec as P

epsilon = 1e-05
send_pieces = 2


def local_stats(values):
    local_peak = jnp.max(values, axis=1)
    local_sum = jnp.sum(jnp.exp(values - local_peak[:, None]), axis=1)
    return jnp.stack([local_peak, local_sum])


def reduce_stats(stats, axis):
    size = lax.axis_size(axis)
    if size & (size - 1):
        gathered = lax.all_gather(stats, axis, axis=0, tiled=False)
        peak = jnp.max(gathered[:, 0], axis=0)
        summed = jnp.sum(gathered[:, 1] * jnp.exp(gathered[:, 0] - peak[None]), axis=0)
        return peak, summed
    distance = 1
    while distance < size:
        perm = [(a, a ^ distance) for a in range(size)]
        other = lax.ppermute(stats, axis, perm)
        peak = jnp.maximum(stats[0], other[0])
        summed = stats[1] * jnp.exp(stats[0] - peak) + other[1] * jnp.exp(other[0] - peak)
        stats = jnp.stack([peak, summed])
        distance *= 2
    return stats[0], stats[1]


def on_device(hidden, norm_gain, head, pool_weight):
    members = lax.axis_size("member")
    shards = lax.axis_size("vocab")
    me = lax.axis_index("member")
    states = hidden[0]
    row_count, width = states.shape
    share = row_count // members
    weights = head[0]
    width_all = width * shards
    w = pool_weight[0]
    sub = share // send_pieces
    gain = None

    def normalize(pieces):
        nonlocal gain
        packed = jnp.concatenate(pieces + ([norm_gain] if gain is None else []), axis=0)
        rows = sum(piece.shape[0] for piece in pieces)
        gathered = lax.all_gather(packed, "vocab", axis=0, tiled=False)
        if gain is None:
            gain = gathered[:, rows, :].astype(jnp.float32)
        full_states = gathered[:, :rows, :].astype(jnp.float32)
        mean_square = jnp.sum(full_states * full_states, axis=(0, 2)) / width_all
        scaling = lax.rsqrt(mean_square + epsilon)
        normed = (full_states * scaling[None, :, None] * gain[:, None, :]).astype(jnp.bfloat16)
        return jnp.transpose(normed, (1, 0, 2)).reshape(rows, width_all)

    source = [states]

    def rows_of(first_row, rows):
        return lax.dynamic_slice_in_dim(source[0], first_row, rows, 0)

    received = []
    sent = []
    own_head = None
    for shift in range(1, members):
        target = (me + shift) % members
        perm = [(g, (g + shift) % members) for g in range(members)]
        parts = []
        for k in range(send_pieces):
            pieces = [rows_of(target * share + k * sub, sub)]
            last = shift == members - 1 and k == send_pieces - 1
            if last:
                pieces.append(rows_of(me * share, 1))
            normed = normalize(pieces)
            if last:
                own_head = normed[sub:]
            logits = jnp.dot(normed[:sub], weights, preferred_element_type=jnp.float32)
            outgoing = w * logits
            if not sent:
                outgoing, source[0] = lax.optimization_barrier((outgoing, states))
            parts.append(lax.ppermute(outgoing, "member", perm))
            sent.append(logits)
        received.append(parts)
    own_normed = jnp.concatenate([own_head, normalize([rows_of(me * share + 1, share - 1)])], axis=0)
    own_logits = jnp.dot(own_normed, weights, preferred_element_type=jnp.float32)

    sent, own_logits = lax.optimization_barrier((sent, own_logits))
    notes = []
    for shift in range(1, members):
        piece_stats = [local_stats(x) for x in sent[(shift - 1) * send_pieces:shift * send_pieces]]
        note = jnp.concatenate(
            [jnp.concatenate(piece_stats, axis=1), jnp.broadcast_to(w, (1, share))], axis=0)
        perm = [(g, (g + shift) % members) for g in range(members)]
        notes.append(lax.ppermute(note, "member", perm))

    def piece_terms(k):
        own = own_logits[k * sub:(k + 1) * sub]
        total = w * own
        for parts in received:
            total = total + parts[k]
        return total, jnp.concatenate([local_stats(own), local_stats(total)], axis=1)

    def flat_lse(stats):
        peak, summed = reduce_stats(stats[:, None, :], "vocab")
        return (peak + jnp.log(summed))[0]

    early = [piece_terms(k) for k in range(send_pieces - 1)]
    early_lse = flat_lse(jnp.concatenate([stats for _, stats in early], axis=1))
    last_parts = [parts[-1] for parts in received]
    last_parts, early_lse = lax.optimization_barrier((last_parts, early_lse))
    for parts, part in zip(received, last_parts):
        parts[-1] = part
    last_total, last_stats = piece_terms(send_pieces - 1)
    tail_lse = flat_lse(jnp.concatenate([last_stats] + [note[:2] for note in notes], axis=1))

    own_lse = []
    pooled_lse = []
    for k in range(send_pieces - 1):
        own_lse.append(early_lse[2 * k * sub:(2 * k + 1) * sub])
        pooled_lse.append(early_lse[(2 * k + 1) * sub:(2 * k + 2) * sub])
    own_lse.append(tail_lse[:sub])
    pooled_lse.append(tail_lse[sub:2 * sub])
    offset = w * jnp.concatenate(own_lse)
    for index, note in enumerate(notes):
        lo = 2 * sub + index * share
        offset = offset + note[2] * tail_lse[lo:lo + share]

    agreement = jnp.concatenate(pooled_lse) - offset
    pooled_raw = jnp.concatenate([total for total, _ in early] + [last_total], axis=0)
    pooled = pooled_raw - offset[:, None]
    return (pooled - agreement[:, None], agreement)


def solution(mesh):
    in_specs = (
        P("member", None, "vocab"),
        P("member", "vocab"),
        P("member", None, "vocab"),
        P("member"),
    )
    out_specs = (P("member", "vocab"), P("member"))
    return jax.shard_map(
        on_device, mesh=mesh, in_specs=in_specs, out_specs=out_specs, check_vma=False
    )
```

```python
import jax
import jax.numpy as jnp
from jax import lax
from jax.sharding import PartitionSpec as P

epsilon = 1e-05
send_pieces = 2


def local_stats(values):
    local_peak = jnp.max(values, axis=1)
    local_sum = jnp.sum(jnp.exp(values - local_peak[:, None]), axis=1)
    return jnp.stack([local_peak, local_sum])


def reduce_stats(stats, axis):
    size = lax.axis_size(axis)
    if size & (size - 1):
        gathered = lax.all_gather(stats, axis, axis=0, tiled=False)
        peak = jnp.max(gathered[:, 0], axis=0)
        summed = jnp.sum(gathered[:, 1] * jnp.exp(gathered[:, 0] - peak[None]), axis=0)
        return peak, summed
    stride = 1
    while stride < size:
        radix = 4 if stride * 4 <= size else 2
        others = [
            lax.ppermute(stats, axis, [(a, a ^ (j * stride)) for a in range(size)])
            for j in range(1, radix)
        ]
        values = [stats] + others
        peak = values[0][0]
        for value in values[1:]:
            peak = jnp.maximum(peak, value[0])
        terms = [value[1] * jnp.exp(value[0] - peak) for value in values]
        if radix == 4:
            summed = (terms[0] + terms[1]) + (terms[2] + terms[3])
        else:
            summed = terms[0] + terms[1]
        stats = jnp.stack([peak, summed])
        stride *= radix
    return stats[0], stats[1]


def on_device(hidden, norm_gain, head, pool_weight):
    members = lax.axis_size("member")
    shards = lax.axis_size("vocab")
    me = lax.axis_index("member")
    states = hidden[0]
    row_count, width = states.shape
    share = row_count // members
    weights = head[0]
    width_all = width * shards
    def logits_of(first_row, rows):
        piece = lax.dynamic_slice_in_dim(states, first_row, rows, 0)
        packed = jnp.concatenate([piece, norm_gain], axis=0)
        gathered = lax.all_gather(packed, "vocab", axis=0, tiled=False)
        full_states = gathered[:, :rows, :].astype(jnp.float32)
        gain = gathered[:, rows, :].astype(jnp.float32)
        mean_square = jnp.sum(full_states * full_states, axis=(0, 2)) / width_all
        scaling = lax.rsqrt(mean_square + epsilon)
        normed = (full_states * scaling[None, :, None] * gain[:, None, :]).astype(jnp.bfloat16)
        normed = jnp.transpose(normed, (1, 0, 2)).reshape(rows, width_all)
        return jnp.dot(normed, weights, preferred_element_type=jnp.float32)

    w = pool_weight[0]
    sub = share // send_pieces
    received = []
    notes = []
    for shift in range(1, members):
        target = (me + shift) % members
        perm = [(g, (g + shift) % members) for g in range(members)]
        parts = []
        piece_stats = []
        for k in range(send_pieces):
            logits = logits_of(target * share + k * sub, sub)
            parts.append(lax.ppermute(w * logits, "member", perm))
            piece_stats.append(local_stats(logits))
        stats_rows = jnp.concatenate(piece_stats, axis=1)
        note = jnp.concatenate([stats_rows, jnp.broadcast_to(w, (1, share))], axis=0)
        received.append(parts)
        notes.append((perm, note))
    own_logits = jnp.concatenate(
        [logits_of(me * share + k * sub, sub) for k in range(send_pieces)], axis=0)
    notes, own_logits = lax.optimization_barrier(([note for _, note in notes], own_logits))
    notes = [lax.ppermute(note, "member", [(g, (g + shift) % members) for g in range(members)])
             for shift, note in zip(range(1, members), notes)]

    pooled_raw = []
    stats = []
    for k in range(send_pieces):
        own = own_logits[k * sub:(k + 1) * sub]
        total = w * own
        for parts in received:
            total = total + parts[k]
        pooled_raw.append(total)
        stats.append(jnp.stack([local_stats(own), local_stats(total)], axis=1))
    stats = jnp.concatenate(stats, axis=2)
    stats = jnp.concatenate([stats] + [note[:2, None, :] for note in notes], axis=1)
    peak, summed = reduce_stats(stats, "vocab")
    lse = peak + jnp.log(summed)
    offset = w * lse[0]
    for index, note in enumerate(notes):
        offset = offset + note[2] * lse[index + 2]

    agreement = lse[1] - offset
    pooled = jnp.concatenate(pooled_raw, axis=0) - offset[:, None]
    return (pooled - agreement[:, None], agreement)


def solution(mesh):
    in_specs = (
        P("member", None, "vocab"),
        P("member", "vocab"),
        P("member", None, "vocab"),
        P("member"),
    )
    out_specs = (P("member", "vocab"), P("member"))
    return jax.shard_map(
        on_device, mesh=mesh, in_specs=in_specs, out_specs=out_specs, check_vma=False
    )
```

```python
import jax
import jax.numpy as jnp
from jax import lax
from jax.sharding import PartitionSpec as P

epsilon = 1e-05
send_pieces = 2


def local_stats(values):
    local_peak = jnp.max(values, axis=1)
    local_sum = jnp.sum(jnp.exp(values - local_peak[:, None]), axis=1)
    return jnp.stack([local_peak, local_sum])


def reduce_stats(stats, axis):
    size = lax.axis_size(axis)
    if size & (size - 1):
        gathered = lax.all_gather(stats, axis, axis=0, tiled=False)
        peak = jnp.max(gathered[:, 0], axis=0)
        summed = jnp.sum(gathered[:, 1] * jnp.exp(gathered[:, 0] - peak[None]), axis=0)
        return peak, summed
    stride = 1
    while stride < size:
        radix = 4 if stride * 4 <= size else 2
        others = [
            lax.ppermute(stats, axis, [(a, a ^ (j * stride)) for a in range(size)])
            for j in range(1, radix)
        ]
        values = [stats] + others
        peak = values[0][0]
        for value in values[1:]:
            peak = jnp.maximum(peak, value[0])
        terms = [value[1] * jnp.exp(value[0] - peak) for value in values]
        if radix == 4:
            summed = (terms[0] + terms[1]) + (terms[2] + terms[3])
        else:
            summed = terms[0] + terms[1]
        stats = jnp.stack([peak, summed])
        stride *= radix
    return stats[0], stats[1]


def on_device(hidden, norm_gain, head, pool_weight):
    members = lax.axis_size("member")
    shards = lax.axis_size("vocab")
    me = lax.axis_index("member")
    states = hidden[0]
    row_count, width = states.shape
    share = row_count // members
    weights = head[0]
    width_all = width * shards
    def normed_of(first_row, rows):
        piece = lax.dynamic_slice_in_dim(states, first_row, rows, 0)
        packed = jnp.concatenate([piece, norm_gain], axis=0)
        gathered = lax.all_gather(packed, "vocab", axis=0, tiled=False)
        full_states = gathered[:, :rows, :].astype(jnp.float32)
        gain = gathered[:, rows, :].astype(jnp.float32)
        mean_square = jnp.sum(full_states * full_states, axis=(0, 2)) / width_all
        scaling = lax.rsqrt(mean_square + epsilon)
        normed = (full_states * scaling[None, :, None] * gain[:, None, :]).astype(jnp.bfloat16)
        return jnp.transpose(normed, (1, 0, 2)).reshape(rows, width_all)

    def logits_of(first_row, rows):
        return jnp.dot(normed_of(first_row, rows), weights, preferred_element_type=jnp.float32)

    w = pool_weight[0]
    sub = share // send_pieces
    received = []
    notes = []
    for shift in range(1, members):
        target = (me + shift) % members
        perm = [(g, (g + shift) % members) for g in range(members)]
        parts = []
        piece_stats = []
        for k in range(send_pieces):
            logits = logits_of(target * share + k * sub, sub)
            parts.append(lax.ppermute(w * logits, "member", perm))
            piece_stats.append(local_stats(logits))
        stats_rows = jnp.concatenate(piece_stats, axis=1)
        note = jnp.concatenate([stats_rows, jnp.broadcast_to(w, (1, share))], axis=0)
        received.append(parts)
        notes.append((perm, note))
    own_normed = jnp.concatenate(
        [normed_of(me * share + k * sub, sub) for k in range(send_pieces)], axis=0)
    own_logits = jnp.dot(own_normed, weights, preferred_element_type=jnp.float32)
    notes, own_logits = lax.optimization_barrier(([note for _, note in notes], own_logits))
    notes = [lax.ppermute(note, "member", [(g, (g + shift) % members) for g in range(members)])
             for shift, note in zip(range(1, members), notes)]

    pooled_raw = []
    stats = []
    for k in range(send_pieces):
        own = own_logits[k * sub:(k + 1) * sub]
        total = w * own
        for parts in received:
            total = total + parts[k]
        pooled_raw.append(total)
        stats.append(jnp.stack([local_stats(own), local_stats(total)], axis=1))
    stats = jnp.concatenate(stats, axis=2)
    stats = jnp.concatenate([stats] + [note[:2, None, :] for note in notes], axis=1)
    peak, summed = reduce_stats(stats, "vocab")
    lse = peak + jnp.log(summed)
    offset = w * lse[0]
    for index, note in enumerate(notes):
        offset = offset + note[2] * lse[index + 2]

    agreement = lse[1] - offset
    pooled = jnp.concatenate(pooled_raw, axis=0) - offset[:, None]
    return (pooled - agreement[:, None], agreement)


def solution(mesh):
    in_specs = (
        P("member", None, "vocab"),
        P("member", "vocab"),
        P("member", None, "vocab"),
        P("member"),
    )
    out_specs = (P("member", "vocab"), P("member"))
    return jax.shard_map(
        on_device, mesh=mesh, in_specs=in_specs, out_specs=out_specs, check_vma=False
    )
```

```python
import jax
import jax.numpy as jnp
from jax import lax
from jax.sharding import PartitionSpec as P

epsilon = 1e-05
send_pieces = 2


def local_stats(values):
    local_peak = jnp.max(values, axis=1)
    local_sum = jnp.sum(jnp.exp(values - local_peak[:, None]), axis=1)
    return jnp.stack([local_peak, local_sum])


def reduce_stats(stats, axis):
    size = lax.axis_size(axis)
    if size & (size - 1):
        gathered = lax.all_gather(stats, axis, axis=0, tiled=False)
        peak = jnp.max(gathered[:, 0], axis=0)
        summed = jnp.sum(gathered[:, 1] * jnp.exp(gathered[:, 0] - peak[None]), axis=0)
        return peak, summed
    stride = 1
    while stride < size:
        radix = 4 if stride * 4 <= size else 2
        others = [
            lax.ppermute(stats, axis, [(a, a ^ (j * stride)) for a in range(size)])
            for j in range(1, radix)
        ]
        values = [stats] + others
        peak = values[0][0]
        for value in values[1:]:
            peak = jnp.maximum(peak, value[0])
        terms = [value[1] * jnp.exp(value[0] - peak) for value in values]
        if radix == 4:
            summed = (terms[0] + terms[1]) + (terms[2] + terms[3])
        else:
            summed = terms[0] + terms[1]
        stats = jnp.stack([peak, summed])
        stride *= radix
    return stats[0], stats[1]


def on_device(hidden, norm_gain, head, pool_weight):
    members = lax.axis_size("member")
    shards = lax.axis_size("vocab")
    me = lax.axis_index("member")
    states = hidden[0]
    row_count, width = states.shape
    share = row_count // members
    weights = head[0]
    width_all = width * shards
    def normed_of(first_row, rows):
        piece = lax.dynamic_slice_in_dim(states, first_row, rows, 0)
        packed = jnp.concatenate([piece, norm_gain], axis=0)
        gathered = lax.all_gather(packed, "vocab", axis=0, tiled=False)
        full_states = gathered[:, :rows, :].astype(jnp.float32)
        gain = gathered[:, rows, :].astype(jnp.float32)
        mean_square = jnp.sum(full_states * full_states, axis=(0, 2)) / width_all
        scaling = lax.rsqrt(mean_square + epsilon)
        normed = (full_states * scaling[None, :, None] * gain[:, None, :]).astype(jnp.bfloat16)
        return jnp.transpose(normed, (1, 0, 2)).reshape(rows, width_all)

    def logits_of(first_row, rows):
        return jnp.dot(normed_of(first_row, rows), weights, preferred_element_type=jnp.float32)

    w = pool_weight[0]
    sub = share // send_pieces
    received = []
    notes = []
    for shift in range(1, members):
        target = (me + shift) % members
        perm = [(g, (g + shift) % members) for g in range(members)]
        parts = []
        sent = []
        for k in range(send_pieces):
            logits = logits_of(target * share + k * sub, sub)
            parts.append(lax.ppermute(w * logits, "member", perm))
            sent.append(logits)
        received.append(parts)
        notes.append(sent)
    own_normed = jnp.concatenate(
        [normed_of(me * share + k * sub, sub) for k in range(send_pieces)], axis=0)
    own_logits = jnp.dot(own_normed, weights, preferred_element_type=jnp.float32)
    notes, own_logits = lax.optimization_barrier((notes, own_logits))
    notes = [
        jnp.concatenate([jnp.concatenate([local_stats(x) for x in sent], axis=1),
                         jnp.broadcast_to(w, (1, share))], axis=0)
        for sent in notes
    ]
    notes = [lax.ppermute(note, "member", [(g, (g + shift) % members) for g in range(members)])
             for shift, note in zip(range(1, members), notes)]

    pooled_raw = []
    stats = []
    for k in range(send_pieces):
        own = own_logits[k * sub:(k + 1) * sub]
        total = w * own
        for parts in received:
            total = total + parts[k]
        pooled_raw.append(total)
        stats.append(jnp.stack([local_stats(own), local_stats(total)], axis=1))
    stats = jnp.concatenate(stats, axis=2)
    stats = jnp.concatenate([stats] + [note[:2, None, :] for note in notes], axis=1)
    peak, summed = reduce_stats(stats, "vocab")
    lse = peak + jnp.log(summed)
    offset = w * lse[0]
    for index, note in enumerate(notes):
        offset = offset + note[2] * lse[index + 2]

    agreement = lse[1] - offset
    pooled = jnp.concatenate(pooled_raw, axis=0) - offset[:, None]
    return (pooled - agreement[:, None], agreement)


def solution(mesh):
    in_specs = (
        P("member", None, "vocab"),
        P("member", "vocab"),
        P("member", None, "vocab"),
        P("member"),
    )
    out_specs = (P("member", "vocab"), P("member"))
    return jax.shard_map(
        on_device, mesh=mesh, in_specs=in_specs, out_specs=out_specs, check_vma=False
    )
```

```python
import jax
import jax.numpy as jnp
from jax import lax
from jax.sharding import PartitionSpec as P

epsilon = 1e-05
send_pieces = 2


def local_stats(values):
    local_peak = jnp.max(values, axis=1)
    local_sum = jnp.sum(jnp.exp(values - local_peak[:, None]), axis=1)
    return jnp.stack([local_peak, local_sum])


def reduce_stats(stats, axis):
    size = lax.axis_size(axis)
    if size & (size - 1):
        gathered = lax.all_gather(stats, axis, axis=0, tiled=False)
        peak = jnp.max(gathered[:, 0], axis=0)
        summed = jnp.sum(gathered[:, 1] * jnp.exp(gathered[:, 0] - peak[None]), axis=0)
        return peak, summed
    stride = 1
    while stride < size:
        radix = 4 if stride * 4 <= size else 2
        others = [
            lax.ppermute(stats, axis, [(a, a ^ (j * stride)) for a in range(size)])
            for j in range(1, radix)
        ]
        values = [stats] + others
        peak = values[0][0]
        for value in values[1:]:
            peak = jnp.maximum(peak, value[0])
        terms = [value[1] * jnp.exp(value[0] - peak) for value in values]
        if radix == 4:
            summed = (terms[0] + terms[1]) + (terms[2] + terms[3])
        else:
            summed = terms[0] + terms[1]
        stats = jnp.stack([peak, summed])
        stride *= radix
    return stats[0], stats[1]


def on_device(hidden, norm_gain, head, pool_weight):
    members = lax.axis_size("member")
    shards = lax.axis_size("vocab")
    me = lax.axis_index("member")
    states = hidden[0]
    row_count, width = states.shape
    share = row_count // members
    weights = head[0]
    width_all = width * shards
    def normed_of(first_row, rows):
        piece = lax.dynamic_slice_in_dim(states, first_row, rows, 0)
        packed = jnp.concatenate([piece, norm_gain], axis=0)
        gathered = lax.all_gather(packed, "vocab", axis=0, tiled=False)
        full_states = gathered[:, :rows, :].astype(jnp.float32)
        gain = gathered[:, rows, :].astype(jnp.float32)
        mean_square = jnp.sum(full_states * full_states, axis=(0, 2)) / width_all
        scaling = lax.rsqrt(mean_square + epsilon)
        normed = (full_states * scaling[None, :, None] * gain[:, None, :]).astype(jnp.bfloat16)
        return jnp.transpose(normed, (1, 0, 2)).reshape(rows, width_all)

    def logits_of(first_row, rows):
        return jnp.dot(normed_of(first_row, rows), weights, preferred_element_type=jnp.float32)

    w = pool_weight[0]
    sub = share // send_pieces
    received = []
    notes = []
    for shift in range(1, members):
        target = (me + shift) % members
        perm = [(g, (g + shift) % members) for g in range(members)]
        parts = []
        piece_stats = []
        for k in range(send_pieces):
            if shift == 1 and k == 0:
                normed = normed_of(target * share, sub)
                half = weights.shape[1] // 2
                halves = [jnp.dot(normed, columns, preferred_element_type=jnp.float32)
                          for columns in (weights[:, :half], weights[:, half:])]
                sent_halves = [lax.ppermute(w * x, "member", perm) for x in halves]
                parts.append(jnp.concatenate(sent_halves, axis=1))
                piece_stats.append(local_stats(jnp.concatenate(halves, axis=1)))
                continue
            logits = logits_of(target * share + k * sub, sub)
            parts.append(lax.ppermute(w * logits, "member", perm))
            piece_stats.append(local_stats(logits))
        stats_rows = jnp.concatenate(piece_stats, axis=1)
        note = jnp.concatenate([stats_rows, jnp.broadcast_to(w, (1, share))], axis=0)
        received.append(parts)
        notes.append((perm, note))
    own_normed = jnp.concatenate(
        [normed_of(me * share + k * sub, sub) for k in range(send_pieces)], axis=0)
    own_logits = jnp.dot(own_normed, weights, preferred_element_type=jnp.float32)
    notes, own_logits = lax.optimization_barrier(([note for _, note in notes], own_logits))
    notes = [lax.ppermute(note, "member", [(g, (g + shift) % members) for g in range(members)])
             for shift, note in zip(range(1, members), notes)]

    pooled_raw = []
    stats = []
    for k in range(send_pieces):
        own = own_logits[k * sub:(k + 1) * sub]
        total = w * own
        for parts in received:
            total = total + parts[k]
        pooled_raw.append(total)
        stats.append(jnp.stack([local_stats(own), local_stats(total)], axis=1))
    stats = jnp.concatenate(stats, axis=2)
    stats = jnp.concatenate([stats] + [note[:2, None, :] for note in notes], axis=1)
    peak, summed = reduce_stats(stats, "vocab")
    lse = peak + jnp.log(summed)
    offset = w * lse[0]
    for index, note in enumerate(notes):
        offset = offset + note[2] * lse[index + 2]

    agreement = lse[1] - offset
    pooled = jnp.concatenate(pooled_raw, axis=0) - offset[:, None]
    return (pooled - agreement[:, None], agreement)


def solution(mesh):
    in_specs = (
        P("member", None, "vocab"),
        P("member", "vocab"),
        P("member", None, "vocab"),
        P("member"),
    )
    out_specs = (P("member", "vocab"), P("member"))
    return jax.shard_map(
        on_device, mesh=mesh, in_specs=in_specs, out_specs=out_specs, check_vma=False
    )
```

```python
import jax
import jax.numpy as jnp
from jax import lax
from jax.sharding import PartitionSpec as P

epsilon = 1e-05
send_pieces = 2


def local_stats(values):
    local_peak = jnp.max(values, axis=1)
    local_sum = jnp.sum(jnp.exp(values - local_peak[:, None]), axis=1)
    return jnp.stack([local_peak, local_sum])


def reduce_stats(stats, axis):
    size = lax.axis_size(axis)
    if size & (size - 1):
        gathered = lax.all_gather(stats, axis, axis=0, tiled=False)
        peak = jnp.max(gathered[:, 0], axis=0)
        summed = jnp.sum(gathered[:, 1] * jnp.exp(gathered[:, 0] - peak[None]), axis=0)
        return peak, summed
    stride = 1
    while stride < size:
        radix = 4 if stride * 4 <= size else 2
        others = [
            lax.ppermute(stats, axis, [(a, a ^ (j * stride)) for a in range(size)])
            for j in range(1, radix)
        ]
        values = [stats] + others
        peak = values[0][0]
        for value in values[1:]:
            peak = jnp.maximum(peak, value[0])
        terms = [value[1] * jnp.exp(value[0] - peak) for value in values]
        if radix == 4:
            summed = (terms[0] + terms[1]) + (terms[2] + terms[3])
        else:
            summed = terms[0] + terms[1]
        stats = jnp.stack([peak, summed])
        stride *= radix
    return stats[0], stats[1]


def on_device(hidden, norm_gain, head, pool_weight):
    members = lax.axis_size("member")
    shards = lax.axis_size("vocab")
    me = lax.axis_index("member")
    states = hidden[0]
    row_count, width = states.shape
    share = row_count // members
    weights = head[0]
    width_all = width * shards
    gain = None
    source = [states]

    def normed_of(slices):
        nonlocal gain
        pieces = [lax.dynamic_slice_in_dim(source[0], lo, rows, 0) for lo, rows in slices]
        rows = sum(rows for _, rows in slices)
        packed = jnp.concatenate(pieces + ([norm_gain] if gain is None else []), axis=0)
        gathered = lax.all_gather(packed, "vocab", axis=0, tiled=False)
        if gain is None:
            gain = gathered[:, rows, :].astype(jnp.float32)
        full_states = gathered[:, :rows, :].astype(jnp.float32)
        mean_square = jnp.sum(full_states * full_states, axis=(0, 2)) / width_all
        scaling = lax.rsqrt(mean_square + epsilon)
        normed = (full_states * scaling[None, :, None] * gain[:, None, :]).astype(jnp.bfloat16)
        return jnp.transpose(normed, (1, 0, 2)).reshape(rows, width_all)

    w = pool_weight[0]
    sub = share // send_pieces
    received = []
    notes = []
    own_first = None
    for shift in range(1, members):
        target = (me + shift) % members
        perm = [(g, (g + shift) % members) for g in range(members)]
        parts = []
        piece_stats = []
        for k in range(send_pieces):
            slices = [(target * share + k * sub, sub)]
            last = shift == members - 1 and k == send_pieces - 1
            if last:
                slices.append((me * share, 1))
            normed = normed_of(slices)
            if last:
                own_first = normed[sub:]
                normed = normed[:sub]
            if shift == 1 and k == 0:
                half = weights.shape[1] // 2
                halves = [jnp.dot(normed, columns, preferred_element_type=jnp.float32)
                          for columns in (weights[:, :half], weights[:, half:])]
                outgoing = [w * x for x in halves]
                outgoing[0], source[0] = lax.optimization_barrier((outgoing[0], states))
                sent_halves = [lax.ppermute(x, "member", perm) for x in outgoing]
                parts.append(jnp.concatenate(sent_halves, axis=1))
                piece_stats.append(local_stats(jnp.concatenate(halves, axis=1)))
                continue
            logits = jnp.dot(normed, weights, preferred_element_type=jnp.float32)
            parts.append(lax.ppermute(w * logits, "member", perm))
            piece_stats.append(local_stats(logits))
        stats_rows = jnp.concatenate(piece_stats, axis=1)
        note = jnp.concatenate([stats_rows, jnp.broadcast_to(w, (1, share))], axis=0)
        received.append(parts)
        notes.append((perm, note))
    own_normed = jnp.concatenate([own_first, normed_of([(me * share + 1, share - 1)])], axis=0)
    own_logits = jnp.dot(own_normed, weights, preferred_element_type=jnp.float32)
    notes, own_logits = lax.optimization_barrier(([note for _, note in notes], own_logits))
    notes = [lax.ppermute(note, "member", [(g, (g + shift) % members) for g in range(members)])
             for shift, note in zip(range(1, members), notes)]

    pooled_raw = []
    stats = []
    for k in range(send_pieces):
        own = own_logits[k * sub:(k + 1) * sub]
        total = w * own
        for parts in received:
            total = total + parts[k]
        pooled_raw.append(total)
        stats.append(jnp.stack([local_stats(own), local_stats(total)], axis=1))
    stats = jnp.concatenate(stats, axis=2)
    stats = jnp.concatenate([stats] + [note[:2, None, :] for note in notes], axis=1)
    peak, summed = reduce_stats(stats, "vocab")
    lse = peak + jnp.log(summed)
    offset = w * lse[0]
    for index, note in enumerate(notes):
        offset = offset + note[2] * lse[index + 2]

    agreement = lse[1] - offset
    pooled = jnp.concatenate(pooled_raw, axis=0) - offset[:, None]
    return (pooled - agreement[:, None], agreement)


def solution(mesh):
    in_specs = (
        P("member", None, "vocab"),
        P("member", "vocab"),
        P("member", None, "vocab"),
        P("member"),
    )
    out_specs = (P("member", "vocab"), P("member"))
    return jax.shard_map(
        on_device, mesh=mesh, in_specs=in_specs, out_specs=out_specs, check_vma=False
    )
```

```python
import jax
import jax.numpy as jnp
from jax import lax
from jax.sharding import PartitionSpec as P

epsilon = 1e-05
send_pieces = 2


def local_stats(values):
    local_peak = jnp.max(values, axis=1)
    local_sum = jnp.sum(jnp.exp(values - local_peak[:, None]), axis=1)
    return jnp.stack([local_peak, local_sum])


def reduce_stats(stats, axis):
    size = lax.axis_size(axis)
    if size & (size - 1):
        gathered = lax.all_gather(stats, axis, axis=0, tiled=False)
        peak = jnp.max(gathered[:, 0], axis=0)
        summed = jnp.sum(gathered[:, 1] * jnp.exp(gathered[:, 0] - peak[None]), axis=0)
        return peak, summed
    stride = 1
    while stride < size:
        radix = 4 if stride * 4 <= size else 2
        others = [
            lax.ppermute(stats, axis, [(a, a ^ (j * stride)) for a in range(size)])
            for j in range(1, radix)
        ]
        values = [stats] + others
        peak = values[0][0]
        for value in values[1:]:
            peak = jnp.maximum(peak, value[0])
        terms = [value[1] * jnp.exp(value[0] - peak) for value in values]
        if radix == 4:
            summed = (terms[0] + terms[1]) + (terms[2] + terms[3])
        else:
            summed = terms[0] + terms[1]
        stats = jnp.stack([peak, summed])
        stride *= radix
    return stats[0], stats[1]


def on_device(hidden, norm_gain, head, pool_weight):
    members = lax.axis_size("member")
    shards = lax.axis_size("vocab")
    me = lax.axis_index("member")
    states = hidden[0]
    row_count, width = states.shape
    share = row_count // members
    weights = head[0]
    width_all = width * shards
    gain = None
    source = [states]

    def normed_of(slices):
        nonlocal gain
        pieces = [lax.dynamic_slice_in_dim(source[0], lo, rows, 0) for lo, rows in slices]
        rows = sum(rows for _, rows in slices)
        packed = jnp.concatenate(pieces + ([norm_gain] if gain is None else []), axis=0)
        gathered = lax.all_gather(packed, "vocab", axis=0, tiled=False)
        if gain is None:
            gain = gathered[:, rows, :].astype(jnp.float32)
        full_states = gathered[:, :rows, :].astype(jnp.float32)
        mean_square = jnp.sum(full_states * full_states, axis=(0, 2)) / width_all
        scaling = lax.rsqrt(mean_square + epsilon)
        normed = (full_states * scaling[None, :, None] * gain[:, None, :]).astype(jnp.bfloat16)
        return jnp.transpose(normed, (1, 0, 2)).reshape(rows, width_all)

    w = pool_weight[0]
    sub = share // send_pieces
    received = []
    notes = []
    own_first = None
    for shift in range(1, members):
        target = (me + shift) % members
        perm = [(g, (g + shift) % members) for g in range(members)]
        parts = []
        piece_stats = []
        for k in range(send_pieces):
            slices = [(target * share + k * sub, sub)]
            last = shift == members - 1 and k == send_pieces - 1
            if last:
                slices.append((me * share, 1))
            normed = normed_of(slices)
            if last:
                own_first = normed[sub:]
                normed = normed[:sub]
            if shift == 1 and k == 0:
                half = weights.shape[1] // 2
                halves = [jnp.dot(normed, columns, preferred_element_type=jnp.float32)
                          for columns in (weights[:, :half], weights[:, half:])]
                outgoing = [w * x for x in halves]
                outgoing[0], source[0] = lax.optimization_barrier((outgoing[0], states))
                sent_halves = [lax.ppermute(x, "member", perm) for x in outgoing]
                parts.append(jnp.concatenate(sent_halves, axis=1))
                piece_stats.append(local_stats(jnp.concatenate(halves, axis=1)))
                continue
            logits = jnp.dot(normed, weights, preferred_element_type=jnp.float32)
            parts.append(lax.ppermute(w * logits, "member", perm))
            piece_stats.append(local_stats(logits))
        stats_rows = jnp.concatenate(piece_stats, axis=1)
        note = jnp.concatenate([stats_rows, jnp.broadcast_to(w, (1, share))], axis=0)
        received.append(parts)
        notes.append((perm, note))
    own_normed = jnp.concatenate([own_first, normed_of([(me * share + 1, share - 1)])], axis=0)
    own_logits = jnp.dot(own_normed, weights, preferred_element_type=jnp.float32)
    notes, own_logits = lax.optimization_barrier(([note for _, note in notes], own_logits))
    notes = [lax.ppermute(note, "member", [(g, (g + shift) % members) for g in range(members)])
             for shift, note in zip(range(1, members), notes)]

    def piece_terms(k):
        own = own_logits[k * sub:(k + 1) * sub]
        total = w * own
        for parts in received:
            total = total + parts[k]
        return total, jnp.concatenate([local_stats(own), local_stats(total)], axis=1)

    def flat_lse(stats):
        peak, summed = reduce_stats(stats[:, None, :], "vocab")
        return (peak + jnp.log(summed))[0]

    early = [piece_terms(k) for k in range(send_pieces - 1)]
    early_lse = flat_lse(jnp.concatenate([stats for _, stats in early], axis=1))
    last_parts = [parts[-1] for parts in received]
    last_parts, early_lse = lax.optimization_barrier((last_parts, early_lse))
    for parts, part in zip(received, last_parts):
        parts[-1] = part
    last_total, last_stats = piece_terms(send_pieces - 1)
    tail_lse = flat_lse(jnp.concatenate([last_stats] + [note[:2] for note in notes], axis=1))

    own_lse = []
    pooled_lse = []
    for k in range(send_pieces - 1):
        own_lse.append(early_lse[2 * k * sub:(2 * k + 1) * sub])
        pooled_lse.append(early_lse[(2 * k + 1) * sub:(2 * k + 2) * sub])
    own_lse.append(tail_lse[:sub])
    pooled_lse.append(tail_lse[sub:2 * sub])
    offset = w * jnp.concatenate(own_lse)
    for index, note in enumerate(notes):
        lo = 2 * sub + index * share
        offset = offset + note[2] * tail_lse[lo:lo + share]

    agreement = jnp.concatenate(pooled_lse) - offset
    pooled_raw = jnp.concatenate([total for total, _ in early] + [last_total], axis=0)
    pooled = pooled_raw - offset[:, None]
    return (pooled - agreement[:, None], agreement)


def solution(mesh):
    in_specs = (
        P("member", None, "vocab"),
        P("member", "vocab"),
        P("member", None, "vocab"),
        P("member"),
    )
    out_specs = (P("member", "vocab"), P("member"))
    return jax.shard_map(
        on_device, mesh=mesh, in_specs=in_specs, out_specs=out_specs, check_vma=False
    )
```

```python
import jax
import jax.numpy as jnp
from jax import lax
from jax.sharding import PartitionSpec as P

epsilon = 1e-05
send_pieces = 2


def local_stats(values):
    local_peak = jnp.max(values, axis=1)
    local_sum = jnp.sum(jnp.exp(values - local_peak[:, None]), axis=1)
    return jnp.stack([local_peak, local_sum])


def reduce_stats(stats, axis):
    size = lax.axis_size(axis)
    if size & (size - 1):
        gathered = lax.all_gather(stats, axis, axis=0, tiled=False)
        peak = jnp.max(gathered[:, 0], axis=0)
        summed = jnp.sum(gathered[:, 1] * jnp.exp(gathered[:, 0] - peak[None]), axis=0)
        return peak, summed
    stride = 1
    while stride < size:
        radix = 4 if stride * 4 <= size else 2
        others = [
            lax.ppermute(stats, axis, [(a, a ^ (j * stride)) for a in range(size)])
            for j in range(1, radix)
        ]
        values = [stats] + others
        peak = values[0][0]
        for value in values[1:]:
            peak = jnp.maximum(peak, value[0])
        terms = [value[1] * jnp.exp(value[0] - peak) for value in values]
        if radix == 4:
            summed = (terms[0] + terms[1]) + (terms[2] + terms[3])
        else:
            summed = terms[0] + terms[1]
        stats = jnp.stack([peak, summed])
        stride *= radix
    return stats[0], stats[1]


def on_device(hidden, norm_gain, head, pool_weight):
    members = lax.axis_size("member")
    shards = lax.axis_size("vocab")
    me = lax.axis_index("member")
    states = hidden[0]
    row_count, width = states.shape
    share = row_count // members
    weights = head[0]
    width_all = width * shards
    gain = None
    source = [states]

    def normed_of(slices):
        nonlocal gain
        pieces = [lax.dynamic_slice_in_dim(source[0], lo, rows, 0) for lo, rows in slices]
        rows = sum(rows for _, rows in slices)
        packed = jnp.concatenate(pieces + ([norm_gain] if gain is None else []), axis=0)
        gathered = lax.all_gather(packed, "vocab", axis=0, tiled=False)
        if gain is None:
            gain = gathered[:, rows, :].astype(jnp.float32)
        full_states = gathered[:, :rows, :].astype(jnp.float32)
        mean_square = jnp.sum(full_states * full_states, axis=(0, 2)) / width_all
        scaling = lax.rsqrt(mean_square + epsilon)
        normed = (full_states * scaling[None, :, None] * gain[:, None, :]).astype(jnp.bfloat16)
        return jnp.transpose(normed, (1, 0, 2)).reshape(rows, width_all)

    w = pool_weight[0]
    sub = share // send_pieces
    received = []
    notes = []
    own_first = None
    for shift in range(1, members):
        target = (me + shift) % members
        perm = [(g, (g + shift) % members) for g in range(members)]
        parts = []
        piece_stats = []
        for k in range(send_pieces):
            slices = [(target * share + k * sub, sub)]
            last = shift == members - 1 and k == send_pieces - 1
            if last:
                slices.append((me * share, 1))
            normed = normed_of(slices)
            if last:
                own_first = normed[sub:]
                normed = normed[:sub]
            if shift == 1 and k == 0:
                half = (weights.shape[1] // 2 + 127) // 128 * 128
                halves = [jnp.dot(normed, columns, preferred_element_type=jnp.float32)
                          for columns in (weights[:, :half], weights[:, half:])]
                outgoing = [w * x for x in halves]
                outgoing[0], source[0] = lax.optimization_barrier((outgoing[0], states))
                sent_halves = [lax.ppermute(x, "member", perm) for x in outgoing]
                parts.append(jnp.concatenate(sent_halves, axis=1))
                piece_stats.append(local_stats(jnp.concatenate(halves, axis=1)))
                continue
            logits = jnp.dot(normed, weights, preferred_element_type=jnp.float32)
            parts.append(lax.ppermute(w * logits, "member", perm))
            piece_stats.append(local_stats(logits))
        stats_rows = jnp.concatenate(piece_stats, axis=1)
        note = jnp.concatenate([stats_rows, jnp.broadcast_to(w, (1, share))], axis=0)
        received.append(parts)
        notes.append((perm, note))
    own_normed = jnp.concatenate([own_first, normed_of([(me * share + 1, share - 1)])], axis=0)
    own_logits = jnp.dot(own_normed, weights, preferred_element_type=jnp.float32)
    notes, own_logits = lax.optimization_barrier(([note for _, note in notes], own_logits))
    notes = [lax.ppermute(note, "member", [(g, (g + shift) % members) for g in range(members)])
             for shift, note in zip(range(1, members), notes)]

    def piece_terms(k):
        own = own_logits[k * sub:(k + 1) * sub]
        total = w * own
        for parts in received:
            total = total + parts[k]
        return total, jnp.concatenate([local_stats(own), local_stats(total)], axis=1)

    def flat_lse(stats):
        peak, summed = reduce_stats(stats[:, None, :], "vocab")
        return (peak + jnp.log(summed))[0]

    early = [piece_terms(k) for k in range(send_pieces - 1)]
    early_lse = flat_lse(jnp.concatenate([stats for _, stats in early], axis=1))
    last_parts = [parts[-1] for parts in received]
    last_parts, early_lse = lax.optimization_barrier((last_parts, early_lse))
    for parts, part in zip(received, last_parts):
        parts[-1] = part
    last_total, last_stats = piece_terms(send_pieces - 1)
    tail_lse = flat_lse(jnp.concatenate([last_stats] + [note[:2] for note in notes], axis=1))

    own_lse = []
    pooled_lse = []
    for k in range(send_pieces - 1):
        own_lse.append(early_lse[2 * k * sub:(2 * k + 1) * sub])
        pooled_lse.append(early_lse[(2 * k + 1) * sub:(2 * k + 2) * sub])
    own_lse.append(tail_lse[:sub])
    pooled_lse.append(tail_lse[sub:2 * sub])
    offset = w * jnp.concatenate(own_lse)
    for index, note in enumerate(notes):
        lo = 2 * sub + index * share
        offset = offset + note[2] * tail_lse[lo:lo + share]

    agreement = jnp.concatenate(pooled_lse) - offset
    pooled_raw = jnp.concatenate([total for total, _ in early] + [last_total], axis=0)
    pooled = pooled_raw - offset[:, None]
    return (pooled - agreement[:, None], agreement)


def solution(mesh):
    in_specs = (
        P("member", None, "vocab"),
        P("member", "vocab"),
        P("member", None, "vocab"),
        P("member"),
    )
    out_specs = (P("member", "vocab"), P("member"))
    return jax.shard_map(
        on_device, mesh=mesh, in_specs=in_specs, out_specs=out_specs, check_vma=False
    )
```

```python
import jax
import jax.numpy as jnp
from jax import lax
from jax.sharding import PartitionSpec as P

epsilon = 1e-05
send_pieces = 2


def local_stats(values):
    local_peak = jnp.max(values, axis=1)
    local_sum = jnp.sum(jnp.exp(values - local_peak[:, None]), axis=1)
    return jnp.stack([local_peak, local_sum])


def reduce_stats(stats, axis):
    size = lax.axis_size(axis)
    if size & (size - 1):
        gathered = lax.all_gather(stats, axis, axis=0, tiled=False)
        peak = jnp.max(gathered[:, 0], axis=0)
        summed = jnp.sum(gathered[:, 1] * jnp.exp(gathered[:, 0] - peak[None]), axis=0)
        return peak, summed
    stride = 1
    while stride < size:
        radix = 4 if stride * 4 <= size else 2
        others = [
            lax.ppermute(stats, axis, [(a, a ^ (j * stride)) for a in range(size)])
            for j in range(1, radix)
        ]
        values = [stats] + others
        peak = values[0][0]
        for value in values[1:]:
            peak = jnp.maximum(peak, value[0])
        terms = [value[1] * jnp.exp(value[0] - peak) for value in values]
        if radix == 4:
            summed = (terms[0] + terms[1]) + (terms[2] + terms[3])
        else:
            summed = terms[0] + terms[1]
        stats = jnp.stack([peak, summed])
        stride *= radix
    return stats[0], stats[1]


def on_device(hidden, norm_gain, head, pool_weight):
    members = lax.axis_size("member")
    shards = lax.axis_size("vocab")
    me = lax.axis_index("member")
    states = hidden[0]
    row_count, width = states.shape
    share = row_count // members
    weights = head[0]
    width_all = width * shards
    gain = None
    source = [states]

    def normed_of(slices):
        nonlocal gain
        pieces = [lax.dynamic_slice_in_dim(source[0], lo, rows, 0) for lo, rows in slices]
        rows = sum(rows for _, rows in slices)
        packed = jnp.concatenate(pieces + ([norm_gain] if gain is None else []), axis=0)
        gathered = lax.all_gather(packed, "vocab", axis=0, tiled=False)
        if gain is None:
            gain = gathered[:, rows, :].astype(jnp.float32)
        full_states = gathered[:, :rows, :].astype(jnp.float32)
        mean_square = jnp.sum(full_states * full_states, axis=(0, 2)) / width_all
        scaling = lax.rsqrt(mean_square + epsilon)
        normed = (full_states * scaling[None, :, None] * gain[:, None, :]).astype(jnp.bfloat16)
        return jnp.transpose(normed, (1, 0, 2)).reshape(rows, width_all)

    w = pool_weight[0]
    sub = share // send_pieces
    received = []
    notes = []
    own_first = None
    for shift in range(1, members):
        target = (me + shift) % members
        perm = [(g, (g + shift) % members) for g in range(members)]
        parts = []
        piece_stats = []
        for k in range(send_pieces):
            slices = [(target * share + k * sub, sub)]
            last = shift == members - 1 and k == send_pieces - 1
            if last:
                slices.append((me * share, 1))
            normed = normed_of(slices)
            if last:
                own_first = normed[sub:]
                normed = normed[:sub]
            if shift == 1 and k == 0:
                half = weights.shape[1] // 2
                halves = [jnp.dot(normed, columns, preferred_element_type=jnp.float32)
                          for columns in (weights[:, :half], weights[:, half:])]
                outgoing = [w * x for x in halves]
                outgoing[0], source[0] = lax.optimization_barrier((outgoing[0], states))
                sent_halves = [lax.ppermute(x, "member", perm) for x in outgoing]
                parts.append(jnp.concatenate(sent_halves, axis=1))
                piece_stats.append(local_stats(jnp.concatenate(halves, axis=1)))
                continue
            logits = jnp.dot(normed, weights, preferred_element_type=jnp.float32)
            parts.append(lax.ppermute(w * logits, "member", perm))
            piece_stats.append(local_stats(logits))
        stats_rows = jnp.concatenate(piece_stats, axis=1)
        note = jnp.concatenate([stats_rows, jnp.broadcast_to(w, (1, share))], axis=0)
        received.append(parts)
        notes.append(lax.ppermute(note, "member", perm))
    own_normed = jnp.concatenate([own_first, normed_of([(me * share + 1, share - 1)])], axis=0)
    own_logits = jnp.dot(own_normed, weights, preferred_element_type=jnp.float32)

    def piece_terms(k):
        own = own_logits[k * sub:(k + 1) * sub]
        total = w * own
        for parts in received:
            total = total + parts[k]
        return total, jnp.concatenate([local_stats(own), local_stats(total)], axis=1)

    def flat_lse(stats):
        peak, summed = reduce_stats(stats[:, None, :], "vocab")
        return (peak + jnp.log(summed))[0]

    early = [piece_terms(k) for k in range(send_pieces - 1)]
    early_lse = flat_lse(jnp.concatenate([stats for _, stats in early], axis=1))
    last_parts = [parts[-1] for parts in received]
    last_parts, early_lse = lax.optimization_barrier((last_parts, early_lse))
    for parts, part in zip(received, last_parts):
        parts[-1] = part
    last_total, last_stats = piece_terms(send_pieces - 1)
    tail_lse = flat_lse(jnp.concatenate([last_stats] + [note[:2] for note in notes], axis=1))

    own_lse = []
    pooled_lse = []
    for k in range(send_pieces - 1):
        own_lse.append(early_lse[2 * k * sub:(2 * k + 1) * sub])
        pooled_lse.append(early_lse[(2 * k + 1) * sub:(2 * k + 2) * sub])
    own_lse.append(tail_lse[:sub])
    pooled_lse.append(tail_lse[sub:2 * sub])
    offset = w * jnp.concatenate(own_lse)
    for index, note in enumerate(notes):
        lo = 2 * sub + index * share
        offset = offset + note[2] * tail_lse[lo:lo + share]

    agreement = jnp.concatenate(pooled_lse) - offset
    pooled_raw = jnp.concatenate([total for total, _ in early] + [last_total], axis=0)
    pooled = pooled_raw - offset[:, None]
    return (pooled - agreement[:, None], agreement)


def solution(mesh):
    in_specs = (
        P("member", None, "vocab"),
        P("member", "vocab"),
        P("member", None, "vocab"),
        P("member"),
    )
    out_specs = (P("member", "vocab"), P("member"))
    return jax.shard_map(
        on_device, mesh=mesh, in_specs=in_specs, out_specs=out_specs, check_vma=False
    )
```

```python
import jax
import jax.numpy as jnp
from jax import lax
from jax.sharding import PartitionSpec as P

epsilon = 1e-05
send_pieces = 2


def local_stats(values):
    local_peak = jnp.max(values, axis=1)
    local_sum = jnp.sum(jnp.exp(values - local_peak[:, None]), axis=1)
    return jnp.stack([local_peak, local_sum])


def reduce_stats(stats, axis):
    size = lax.axis_size(axis)
    if size & (size - 1):
        gathered = lax.all_gather(stats, axis, axis=0, tiled=False)
        peak = jnp.max(gathered[:, 0], axis=0)
        summed = jnp.sum(gathered[:, 1] * jnp.exp(gathered[:, 0] - peak[None]), axis=0)
        return peak, summed
    stride = 1
    while stride < size:
        radix = 4 if stride == 1 and size >= 4 else 2
        others = [
            lax.ppermute(stats, axis, [(a, a ^ (j * stride)) for a in range(size)])
            for j in range(1, radix)
        ]
        values = [stats] + others
        peak = values[0][0]
        for value in values[1:]:
            peak = jnp.maximum(peak, value[0])
        terms = [value[1] * jnp.exp(value[0] - peak) for value in values]
        if radix == 4:
            summed = (terms[0] + terms[1]) + (terms[2] + terms[3])
        else:
            summed = terms[0] + terms[1]
        stats = jnp.stack([peak, summed])
        stride *= radix
    return stats[0], stats[1]


def on_device(hidden, norm_gain, head, pool_weight):
    members = lax.axis_size("member")
    shards = lax.axis_size("vocab")
    me = lax.axis_index("member")
    states = hidden[0]
    row_count, width = states.shape
    share = row_count // members
    weights = head[0]
    width_all = width * shards
    gain = None
    source = [states]

    def normed_of(slices):
        nonlocal gain
        pieces = [lax.dynamic_slice_in_dim(source[0], lo, rows, 0) for lo, rows in slices]
        rows = sum(rows for _, rows in slices)
        packed = jnp.concatenate(pieces + ([norm_gain] if gain is None else []), axis=0)
        gathered = lax.all_gather(packed, "vocab", axis=0, tiled=False)
        if gain is None:
            gain = gathered[:, rows, :].astype(jnp.float32)
        full_states = gathered[:, :rows, :].astype(jnp.float32)
        mean_square = jnp.sum(full_states * full_states, axis=(0, 2)) / width_all
        scaling = lax.rsqrt(mean_square + epsilon)
        normed = (full_states * scaling[None, :, None] * gain[:, None, :]).astype(jnp.bfloat16)
        return jnp.transpose(normed, (1, 0, 2)).reshape(rows, width_all)

    w = pool_weight[0]
    sub = share // send_pieces
    received = []
    notes = []
    own_first = None
    for shift in range(1, members):
        target = (me + shift) % members
        perm = [(g, (g + shift) % members) for g in range(members)]
        parts = []
        piece_stats = []
        for k in range(send_pieces):
            slices = [(target * share + k * sub, sub)]
            last = shift == members - 1 and k == send_pieces - 1
            if last:
                slices.append((me * share, 1))
            normed = normed_of(slices)
            if last:
                own_first = normed[sub:]
                normed = normed[:sub]
            if shift == 1 and k == 0:
                half = weights.shape[1] // 2
                halves = [jnp.dot(normed, columns, preferred_element_type=jnp.float32)
                          for columns in (weights[:, :half], weights[:, half:])]
                outgoing = [w * x for x in halves]
                outgoing[0], source[0] = lax.optimization_barrier((outgoing[0], states))
                sent_halves = [lax.ppermute(x, "member", perm) for x in outgoing]
                parts.append(jnp.concatenate(sent_halves, axis=1))
                piece_stats.append(local_stats(jnp.concatenate(halves, axis=1)))
                continue
            logits = jnp.dot(normed, weights, preferred_element_type=jnp.float32)
            parts.append(lax.ppermute(w * logits, "member", perm))
            piece_stats.append(local_stats(logits))
        stats_rows = jnp.concatenate(piece_stats, axis=1)
        note = jnp.concatenate([stats_rows, jnp.broadcast_to(w, (1, share))], axis=0)
        received.append(parts)
        notes.append((perm, note))
    own_normed = jnp.concatenate([own_first, normed_of([(me * share + 1, share - 1)])], axis=0)
    own_logits = jnp.dot(own_normed, weights, preferred_element_type=jnp.float32)
    notes, own_logits = lax.optimization_barrier(([note for _, note in notes], own_logits))
    notes = [lax.ppermute(note, "member", [(g, (g + shift) % members) for g in range(members)])
             for shift, note in zip(range(1, members), notes)]

    def piece_terms(k):
        own = own_logits[k * sub:(k + 1) * sub]
        total = w * own
        for parts in received:
            total = total + parts[k]
        return total, jnp.concatenate([local_stats(own), local_stats(total)], axis=1)

    def flat_lse(stats):
        peak, summed = reduce_stats(stats[:, None, :], "vocab")
        return (peak + jnp.log(summed))[0]

    early = [piece_terms(k) for k in range(send_pieces - 1)]
    early_lse = flat_lse(jnp.concatenate([stats for _, stats in early], axis=1))
    last_parts = [parts[-1] for parts in received]
    last_parts, early_lse = lax.optimization_barrier((last_parts, early_lse))
    for parts, part in zip(received, last_parts):
        parts[-1] = part
    last_total, last_stats = piece_terms(send_pieces - 1)
    tail_lse = flat_lse(jnp.concatenate([last_stats] + [note[:2] for note in notes], axis=1))

    own_lse = []
    pooled_lse = []
    for k in range(send_pieces - 1):
        own_lse.append(early_lse[2 * k * sub:(2 * k + 1) * sub])
        pooled_lse.append(early_lse[(2 * k + 1) * sub:(2 * k + 2) * sub])
    own_lse.append(tail_lse[:sub])
    pooled_lse.append(tail_lse[sub:2 * sub])
    offset = w * jnp.concatenate(own_lse)
    for index, note in enumerate(notes):
        lo = 2 * sub + index * share
        offset = offset + note[2] * tail_lse[lo:lo + share]

    agreement = jnp.concatenate(pooled_lse) - offset
    pooled_raw = jnp.concatenate([total for total, _ in early] + [last_total], axis=0)
    pooled = pooled_raw - offset[:, None]
    return (pooled - agreement[:, None], agreement)


def solution(mesh):
    in_specs = (
        P("member", None, "vocab"),
        P("member", "vocab"),
        P("member", None, "vocab"),
        P("member"),
    )
    out_specs = (P("member", "vocab"), P("member"))
    return jax.shard_map(
        on_device, mesh=mesh, in_specs=in_specs, out_specs=out_specs, check_vma=False
    )
```

```python
import jax
import jax.numpy as jnp
from jax import lax
from jax.sharding import PartitionSpec as P

epsilon = 1e-05
send_pieces = 2


def local_stats(values):
    local_peak = jnp.max(values, axis=1)
    local_sum = jnp.sum(jnp.exp(values - local_peak[:, None]), axis=1)
    return jnp.stack([local_peak, local_sum])


def reduce_stats(stats, axis):
    size = lax.axis_size(axis)
    if size & (size - 1):
        gathered = lax.all_gather(stats, axis, axis=0, tiled=False)
        peak = jnp.max(gathered[:, 0], axis=0)
        summed = jnp.sum(gathered[:, 1] * jnp.exp(gathered[:, 0] - peak[None]), axis=0)
        return peak, summed
    stride = 1
    while stride < size:
        radix = min(size // stride, 16)
        others = [
            lax.ppermute(stats, axis, [(a, a ^ (j * stride)) for a in range(size)])
            for j in range(1, radix)
        ]
        values = [stats] + others
        peak = values[0][0]
        for value in values[1:]:
            peak = jnp.maximum(peak, value[0])
        terms = [value[1] * jnp.exp(value[0] - peak) for value in values]
        while len(terms) > 1:
            terms = [terms[j] + terms[j + 1] for j in range(0, len(terms), 2)]
        stats = jnp.stack([peak, terms[0]])
        stride *= radix
    return stats[0], stats[1]


def on_device(hidden, norm_gain, head, pool_weight):
    members = lax.axis_size("member")
    shards = lax.axis_size("vocab")
    me = lax.axis_index("member")
    states = hidden[0]
    row_count, width = states.shape
    share = row_count // members
    weights = head[0]
    width_all = width * shards
    gain = None
    source = [states]

    def normed_of(slices):
        nonlocal gain
        pieces = [lax.dynamic_slice_in_dim(source[0], lo, rows, 0) for lo, rows in slices]
        rows = sum(rows for _, rows in slices)
        packed = jnp.concatenate(pieces + ([norm_gain] if gain is None else []), axis=0)
        gathered = lax.all_gather(packed, "vocab", axis=0, tiled=False)
        if gain is None:
            gain = gathered[:, rows, :].astype(jnp.float32)
        full_states = gathered[:, :rows, :].astype(jnp.float32)
        mean_square = jnp.sum(full_states * full_states, axis=(0, 2)) / width_all
        scaling = lax.rsqrt(mean_square + epsilon)
        normed = (full_states * scaling[None, :, None] * gain[:, None, :]).astype(jnp.bfloat16)
        return jnp.transpose(normed, (1, 0, 2)).reshape(rows, width_all)

    w = pool_weight[0]
    sub = share // send_pieces
    received = []
    notes = []
    own_first = None
    for shift in range(1, members):
        target = (me + shift) % members
        perm = [(g, (g + shift) % members) for g in range(members)]
        parts = []
        piece_stats = []
        for k in range(send_pieces):
            slices = [(target * share + k * sub, sub)]
            last = shift == members - 1 and k == send_pieces - 1
            if last:
                slices.append((me * share, 1))
            normed = normed_of(slices)
            if last:
                own_first = normed[sub:]
                normed = normed[:sub]
            if shift == 1 and k == 0:
                half = weights.shape[1] // 2
                halves = [jnp.dot(normed, columns, preferred_element_type=jnp.float32)
                          for columns in (weights[:, :half], weights[:, half:])]
                outgoing = [w * x for x in halves]
                outgoing[0], source[0] = lax.optimization_barrier((outgoing[0], states))
                sent_halves = [lax.ppermute(x, "member", perm) for x in outgoing]
                parts.append(jnp.concatenate(sent_halves, axis=1))
                piece_stats.append(local_stats(jnp.concatenate(halves, axis=1)))
                continue
            logits = jnp.dot(normed, weights, preferred_element_type=jnp.float32)
            parts.append(lax.ppermute(w * logits, "member", perm))
            piece_stats.append(local_stats(logits))
        stats_rows = jnp.concatenate(piece_stats, axis=1)
        note = jnp.concatenate([stats_rows, jnp.broadcast_to(w, (1, share))], axis=0)
        received.append(parts)
        notes.append((perm, note))
    own_normed = jnp.concatenate([own_first, normed_of([(me * share + 1, share - 1)])], axis=0)
    own_logits = jnp.dot(own_normed, weights, preferred_element_type=jnp.float32)
    notes, own_logits = lax.optimization_barrier(([note for _, note in notes], own_logits))
    notes = [lax.ppermute(note, "member", [(g, (g + shift) % members) for g in range(members)])
             for shift, note in zip(range(1, members), notes)]

    def piece_terms(k):
        own = own_logits[k * sub:(k + 1) * sub]
        total = w * own
        for parts in received:
            total = total + parts[k]
        return total, jnp.concatenate([local_stats(own), local_stats(total)], axis=1)

    def flat_lse(stats):
        peak, summed = reduce_stats(stats[:, None, :], "vocab")
        return (peak + jnp.log(summed))[0]

    early = [piece_terms(k) for k in range(send_pieces - 1)]
    early_lse = flat_lse(jnp.concatenate([stats for _, stats in early], axis=1))
    last_parts = [parts[-1] for parts in received]
    last_parts, early_lse = lax.optimization_barrier((last_parts, early_lse))
    for parts, part in zip(received, last_parts):
        parts[-1] = part
    last_total, last_stats = piece_terms(send_pieces - 1)
    tail_lse = flat_lse(jnp.concatenate([last_stats] + [note[:2] for note in notes], axis=1))

    own_lse = []
    pooled_lse = []
    for k in range(send_pieces - 1):
        own_lse.append(early_lse[2 * k * sub:(2 * k + 1) * sub])
        pooled_lse.append(early_lse[(2 * k + 1) * sub:(2 * k + 2) * sub])
    own_lse.append(tail_lse[:sub])
    pooled_lse.append(tail_lse[sub:2 * sub])
    offset = w * jnp.concatenate(own_lse)
    for index, note in enumerate(notes):
        lo = 2 * sub + index * share
        offset = offset + note[2] * tail_lse[lo:lo + share]

    agreement = jnp.concatenate(pooled_lse) - offset
    pooled_raw = jnp.concatenate([total for total, _ in early] + [last_total], axis=0)
    pooled = pooled_raw - offset[:, None]
    return (pooled - agreement[:, None], agreement)


def solution(mesh):
    in_specs = (
        P("member", None, "vocab"),
        P("member", "vocab"),
        P("member", None, "vocab"),
        P("member"),
    )
    out_specs = (P("member", "vocab"), P("member"))
    return jax.shard_map(
        on_device, mesh=mesh, in_specs=in_specs, out_specs=out_specs, check_vma=False
    )
```

```python
import jax
import jax.numpy as jnp
from jax import lax
from jax.sharding import PartitionSpec as P

epsilon = 1e-05
send_pieces = 2


def local_stats(values):
    local_peak = jnp.max(values, axis=1)
    local_sum = jnp.sum(jnp.exp(values - local_peak[:, None]), axis=1)
    return jnp.stack([local_peak, local_sum])


def reduce_stats(stats, axis):
    size = lax.axis_size(axis)
    if size & (size - 1):
        gathered = lax.all_gather(stats, axis, axis=0, tiled=False)
        peak = jnp.max(gathered[:, 0], axis=0)
        summed = jnp.sum(gathered[:, 1] * jnp.exp(gathered[:, 0] - peak[None]), axis=0)
        return peak, summed
    rounds = []
    stride = 1
    while stride < size:
        rounds.append((stride, 4 if stride * 4 <= size else 2))
        stride *= rounds[-1][1]
    for stride, radix in reversed(rounds):
        others = [
            lax.ppermute(stats, axis, [(a, a ^ (j * stride)) for a in range(size)])
            for j in range(1, radix)
        ]
        values = [stats] + others
        peak = values[0][0]
        for value in values[1:]:
            peak = jnp.maximum(peak, value[0])
        terms = [value[1] * jnp.exp(value[0] - peak) for value in values]
        if radix == 4:
            summed = (terms[0] + terms[1]) + (terms[2] + terms[3])
        else:
            summed = terms[0] + terms[1]
        stats = jnp.stack([peak, summed])
    return stats[0], stats[1]


def on_device(hidden, norm_gain, head, pool_weight):
    members = lax.axis_size("member")
    shards = lax.axis_size("vocab")
    me = lax.axis_index("member")
    states = hidden[0]
    row_count, width = states.shape
    share = row_count // members
    weights = head[0]
    width_all = width * shards
    gain = None
    source = [states]

    def normed_of(slices):
        nonlocal gain
        pieces = [lax.dynamic_slice_in_dim(source[0], lo, rows, 0) for lo, rows in slices]
        rows = sum(rows for _, rows in slices)
        packed = jnp.concatenate(pieces + ([norm_gain] if gain is None else []), axis=0)
        gathered = lax.all_gather(packed, "vocab", axis=0, tiled=False)
        if gain is None:
            gain = gathered[:, rows, :].astype(jnp.float32)
        full_states = gathered[:, :rows, :].astype(jnp.float32)
        mean_square = jnp.sum(full_states * full_states, axis=(0, 2)) / width_all
        scaling = lax.rsqrt(mean_square + epsilon)
        normed = (full_states * scaling[None, :, None] * gain[:, None, :]).astype(jnp.bfloat16)
        return jnp.transpose(normed, (1, 0, 2)).reshape(rows, width_all)

    w = pool_weight[0]
    sub = share // send_pieces
    received = []
    notes = []
    own_first = None
    for shift in range(1, members):
        target = (me + shift) % members
        perm = [(g, (g + shift) % members) for g in range(members)]
        parts = []
        piece_stats = []
        for k in range(send_pieces):
            slices = [(target * share + k * sub, sub)]
            last = shift == members - 1 and k == send_pieces - 1
            if last:
                slices.append((me * share, 1))
            normed = normed_of(slices)
            if last:
                own_first = normed[sub:]
                normed = normed[:sub]
            if shift == 1 and k == 0:
                half = weights.shape[1] // 2
                halves = [jnp.dot(normed, columns, preferred_element_type=jnp.float32)
                          for columns in (weights[:, :half], weights[:, half:])]
                outgoing = [w * x for x in halves]
                outgoing[0], source[0] = lax.optimization_barrier((outgoing[0], states))
                sent_halves = [lax.ppermute(x, "member", perm) for x in outgoing]
                parts.append(jnp.concatenate(sent_halves, axis=1))
                piece_stats.append(local_stats(jnp.concatenate(halves, axis=1)))
                continue
            logits = jnp.dot(normed, weights, preferred_element_type=jnp.float32)
            parts.append(lax.ppermute(w * logits, "member", perm))
            piece_stats.append(local_stats(logits))
        stats_rows = jnp.concatenate(piece_stats, axis=1)
        note = jnp.concatenate([stats_rows, jnp.broadcast_to(w, (1, share))], axis=0)
        received.append(parts)
        notes.append((perm, note))
    own_normed = jnp.concatenate([own_first, normed_of([(me * share + 1, share - 1)])], axis=0)
    own_logits = jnp.dot(own_normed, weights, preferred_element_type=jnp.float32)
    notes, own_logits = lax.optimization_barrier(([note for _, note in notes], own_logits))
    notes = [lax.ppermute(note, "member", [(g, (g + shift) % members) for g in range(members)])
             for shift, note in zip(range(1, members), notes)]

    def piece_terms(k):
        own = own_logits[k * sub:(k + 1) * sub]
        total = w * own
        for parts in received:
            total = total + parts[k]
        return total, jnp.concatenate([local_stats(own), local_stats(total)], axis=1)

    def flat_lse(stats):
        peak, summed = reduce_stats(stats[:, None, :], "vocab")
        return (peak + jnp.log(summed))[0]

    early = [piece_terms(k) for k in range(send_pieces - 1)]
    early_lse = flat_lse(jnp.concatenate([stats for _, stats in early], axis=1))
    last_parts = [parts[-1] for parts in received]
    last_parts, early_lse = lax.optimization_barrier((last_parts, early_lse))
    for parts, part in zip(received, last_parts):
        parts[-1] = part
    last_total, last_stats = piece_terms(send_pieces - 1)
    tail_lse = flat_lse(jnp.concatenate([last_stats] + [note[:2] for note in notes], axis=1))

    own_lse = []
    pooled_lse = []
    for k in range(send_pieces - 1):
        own_lse.append(early_lse[2 * k * sub:(2 * k + 1) * sub])
        pooled_lse.append(early_lse[(2 * k + 1) * sub:(2 * k + 2) * sub])
    own_lse.append(tail_lse[:sub])
    pooled_lse.append(tail_lse[sub:2 * sub])
    offset = w * jnp.concatenate(own_lse)
    for index, note in enumerate(notes):
        lo = 2 * sub + index * share
        offset = offset + note[2] * tail_lse[lo:lo + share]

    agreement = jnp.concatenate(pooled_lse) - offset
    pooled_raw = jnp.concatenate([total for total, _ in early] + [last_total], axis=0)
    pooled = pooled_raw - offset[:, None]
    return (pooled - agreement[:, None], agreement)


def solution(mesh):
    in_specs = (
        P("member", None, "vocab"),
        P("member", "vocab"),
        P("member", None, "vocab"),
        P("member"),
    )
    out_specs = (P("member", "vocab"), P("member"))
    return jax.shard_map(
        on_device, mesh=mesh, in_specs=in_specs, out_specs=out_specs, check_vma=False
    )
```
